256 devices in a mesh: node: 4 (over x), space: 64 (over z, y, core).
Axes of the slice: x: 4, y: 4, z: 8, core: 2. Of those that a mesh axis runs over, the one named last changes fastest.
Arguments:
- snapshots: bfloat16 [512, 128, 8192], P('node', 'space'), may hold values from -8 to 8
- kappa: bfloat16 [128, 8192], P('space'), may hold values from 0.099609375 to 10
Outputs:
- gram: float32 [512, 512], P('node', 'space')
The draws below stay inside these ranges and needn't reach their ends.
All inputs are finite; a program needn't handle non-finite values.
Results may differ from the reference program's by a relative error of at most 0.0003.
Values may be sent and summed in bfloat16 or wider, within the bound.
No kernel may reach another device: no remote copies, remote signals or barrier semaphores. Data moves between devices by JAX's collectives and lax.ppermute only.
A program may use at most 128 MiB of HBM per device.

```python
import math
import jax
import jax.numpy as jnp
from jax import lax

SNAP_DEV = 128
NY = 128
NZ = 64
SNAPS = 512
NX = 128


def draw_snapshots(key, part):
    key_common = jax.random.fold_in(key, 11)
    key_noise = jax.random.fold_in(key, 12)
    key_weight = jax.random.fold_in(key, 13)
    key_planes = jax.random.fold_in(key, 14)
    plane_gain = jax.random.uniform(key_planes, (NX, 1), jnp.float32, 0.4, 1.6)
    common = jnp.clip(jax.random.normal(key_common, (1, NY * NZ), jnp.float32), -2.5, 2.5)
    noise = jnp.clip(jax.random.normal(key_noise, (SNAPS, NX, NY * NZ), jnp.float32), -4.0, 4.0)
    weights = jax.random.uniform(key_weight, (SNAPS, 1, 1), jnp.float32, -1.0, 1.0)
    field = plane_gain * common
    return (weights * field[None] + noise).astype(jnp.bfloat16)


def level_of(key, dims, cuts, low, high):
    factor_of = 1.0
    for position, blocks in cuts:
        steps = jax.random.uniform(jax.random.fold_in(jax.random.fold_in(key, 6), position), (blocks,), jnp.float32, low / len(cuts), high / len(cuts))
        factor_of = factor_of * jnp.repeat(jnp.exp(steps), dims[position] // blocks).reshape((-1,) + (1,) * (len(dims) - 1 - position))
    return factor_of


def setup_inputs(seed: int = 0) -> dict:
    splits = jax.random.split(jax.random.key(seed), 3)
    snapshots = draw_snapshots(jax.random.fold_in(splits[2], 71), 0)
    kappa = jnp.clip(jnp.exp(math.log(10.0) - 4.609084 * jax.random.uniform(splits[1], (NX, NY * NZ), jnp.float32) ** level_of(splits[1], (NX, NY * NZ), ((0, 64),), -0.2, 0.2)), 0.099609375, 10.0).astype(jnp.bfloat16)
    return dict(snapshots=snapshots, kappa=kappa)


def ahead(values, offset):
    tail = jnp.zeros(values.shape[:-1] + (offset,), values.dtype)
    return jnp.concatenate([values[..., offset:], tail], axis=-1)

def behind(values, offset):
    head = jnp.zeros(values.shape[:-1] + (offset,), values.dtype)
    return jnp.concatenate([head, values[..., :-offset]], axis=-1)

def flat_terms(field, kap_mid):
    width = field.shape[-1]
    zpos = jnp.arange(width, dtype=jnp.int32) % NZ
    up_ok = zpos != NZ - 1
    down_ok = zpos != 0
    total = jnp.zeros(field.shape, jnp.float32)
    near = jnp.where(up_ok, ahead(field, 1), 0.0)
    near_k = jnp.where(up_ok, ahead(kap_mid, 1), 0.0)
    total = total + 0.5 * (kap_mid + near_k) * (field - near)
    near = jnp.where(down_ok, behind(field, 1), 0.0)
    near_k = jnp.where(down_ok, behind(kap_mid, 1), 0.0)
    total = total + 0.5 * (kap_mid + near_k) * (field - near)
    total = total + 0.5 * (kap_mid + ahead(kap_mid, NZ)) * (field - ahead(field, NZ))
    total = total + 0.5 * (kap_mid + behind(kap_mid, NZ)) * (field - behind(field, NZ))
    return total

def stiffness(block, kap):
    padded = jnp.pad(block, ((0, 0), (1, 1), (0, 0)))
    kpad = jnp.pad(kap, ((1, 1), (0, 0)))
    total = flat_terms(block, kap)
    total = total + 0.5 * (kap + kpad[:-2]) * (block - padded[:, :-2])
    total = total + 0.5 * (kap + kpad[2:]) * (block - padded[:, 2:])
    return total

def reference(snapshots, kappa):
    kap = kappa.astype(jnp.float32)
    blocks = snapshots.reshape(SNAPS // SNAP_DEV, SNAP_DEV, NX, NY * NZ)
    image = lax.map(lambda b: stiffness(b.astype(jnp.float32), kap).astype(jnp.bfloat16), blocks)
    image = image.reshape(SNAPS, NX * NY * NZ)
    flat = snapshots.reshape(SNAPS, NX * NY * NZ)
    gram = jnp.dot(image, flat.T, preferred_element_type=jnp.float32)
    return gram * jnp.float32(1.0 / math.sqrt(NX * NY * NZ))
```

```python
import math

import jax
import jax.numpy as jnp
from jax import lax
from jax.experimental import pallas as pl
from jax.experimental.pallas import tpu as pltpu
from jax.sharding import PartitionSpec as P

NY = 128
NZ = 64
ROWS = 32


def ahead(values, offset):
    tail = jnp.zeros(values.shape[:-1] + (offset,), values.dtype)
    return jnp.concatenate([values[..., offset:], tail], axis=-1)


def behind(values, offset):
    head = jnp.zeros(values.shape[:-1] + (offset,), values.dtype)
    return jnp.concatenate([head, values[..., :-offset]], axis=-1)


def stencil_kernel(x_ref, below_ref, above_ref, coef_ref, out_ref):
    span = below_ref.shape[1]
    lane = lax.broadcasted_iota(jnp.int32, (1, span), 1)
    zpos = lane % NZ
    up_ok = zpos != NZ - 1
    down_ok = zpos != 0
    inner = (lane >= NZ) & (lane < span - NZ)
    planes = [x_ref[:, p * span:(p + 1) * span].astype(jnp.float32) for p in range(2)]
    below = below_ref[...].astype(jnp.float32)
    above = above_ref[...].astype(jnp.float32)
    for p in range(2):
        v = planes[p]

        def coef(t):
            return coef_ref[t:t + 1, p * span:(p + 1) * span]

        near = jnp.where(up_ok, pltpu.roll(v, span - 1, 1), 0.0)
        total = coef(0) * (v - near)
        near = jnp.where(down_ok, pltpu.roll(v, 1, 1), 0.0)
        total = total + coef(1) * (v - near)
        total = total + coef(2) * (v - pltpu.roll(v, span - NZ, 1))
        total = total + coef(3) * (v - pltpu.roll(v, NZ, 1))
        total = total + coef(4) * (v - (below if p == 0 else planes[0]))
        total = total + coef(5) * (v - (planes[1] if p == 0 else above))
        out_ref[:, p * span:(p + 1) * span] = jnp.where(inner, total, 0.0).astype(out_ref.dtype)


def stencil(field, below, above, coef):
    snaps, width = field.shape
    span = below.shape[1]
    return pl.pallas_call(
        stencil_kernel,
        grid=(snaps // ROWS,),
        in_specs=[
            pl.BlockSpec((ROWS, width), lambda i: (i, 0)),
            pl.BlockSpec((ROWS, span), lambda i: (i, 0)),
            pl.BlockSpec((ROWS, span), lambda i: (i, 0)),
            pl.BlockSpec(coef.shape, lambda i: (0, 0)),
        ],
        out_specs=pl.BlockSpec((ROWS, width), lambda i: (i, 0)),
        out_shape=jax.ShapeDtypeStruct(field.shape, jnp.bfloat16),
    )(field, below, above, coef)


def weights(kap_chunk, kap_below, kap_above):
    span = kap_chunk.shape[-1]
    kc = kap_chunk.astype(jnp.float32)
    zpos = jnp.arange(span, dtype=jnp.int32) % NZ
    k_zp = jnp.where(zpos != NZ - 1, ahead(kc, 1), 0.0)
    k_zm = jnp.where(zpos != 0, behind(kc, 1), 0.0)
    k_xm = jnp.stack([kap_below.astype(jnp.float32), kc[0]])
    k_xp = jnp.stack([kc[1], kap_above.astype(jnp.float32)])
    near = [k_zp, k_zm, ahead(kc, NZ), behind(kc, NZ), k_xm, k_xp]
    return jnp.stack([0.5 * (kc + k) for k in near]).reshape(6, 2 * span)


def space_coords(s):
    return s // 8, (s // 2) % 4, s % 2


def space_index(z, y, c):
    return z * 8 + y * 2 + c


def per_device(snapshots, kappa):
    rows, planes, width = snapshots.shape
    nodes = lax.axis_size("node")
    spaces = lax.axis_size("space")
    me = lax.axis_index("node")
    sp = lax.axis_index("space")
    chunk = width // nodes
    span = chunk + 2 * NZ
    snaps = rows * nodes

    up = [(i, i + 1) for i in range(spaces - 1)]
    down = [(j, i) for i, j in up]

    kpad = jnp.pad(kappa, ((0, 0), (NZ, NZ)))
    kap_chunk = lax.dynamic_slice_in_dim(kpad, me * chunk, span, axis=1)
    kap_below = lax.ppermute(kap_chunk[1], "space", up)
    kap_above = lax.ppermute(kap_chunk[0], "space", down)
    coef = weights(kap_chunk, kap_below, kap_above)

    spad = jnp.pad(snapshots, ((0, 0), (0, 0), (NZ, NZ)))
    pieces = jnp.stack([spad[:, :, q * chunk:q * chunk + span] for q in range(nodes)])
    pieces = pieces.reshape(nodes, rows, planes * span)
    field = lax.all_to_all(pieces, "node", 0, 0, tiled=True).reshape(snaps, planes * span)

    below = lax.ppermute(field[:, span:], "space", up)
    above = lax.ppermute(field[:, :span], "space", down)
    image = stencil(field, below, above, coef)
    part = lax.dot_general(image, field, (((1,), (1,)), ((), ())), preferred_element_type=jnp.float32)

    z, y, c = space_coords(sp)
    part = part.reshape(snaps, 8, 4, 2, 8)
    keep = jnp.take(part, c, axis=3)
    give = jnp.take(part, 1 - c, axis=3)
    pairs = [(s, s ^ 1) for s in range(spaces)]
    acc = (keep + lax.ppermute(give, "space", pairs)).reshape(nodes, rows, 8, 4, 8)

    total = jnp.take(acc, me, axis=0)
    for d in range(1, nodes):
        blk = jnp.take(acc, (me + d) % nodes, axis=0)
        total = total + lax.ppermute(blk, "node", [(i, (i + d) % nodes) for i in range(nodes)])

    acc = jnp.take(total, y, axis=2)
    for d in range(1, 4):
        blk = jnp.take(total, (y + d) % 4, axis=2)
        pairs = []
        for s in range(spaces):
            zz, yy, cc = space_coords(s)
            pairs.append((s, space_index(zz, (yy + d) % 4, cc)))
        acc = acc + lax.ppermute(blk, "space", pairs)

    out = jnp.take(acc, z, axis=1)
    for d in range(1, 8):
        blk = jnp.take(acc, (z + d) % 8, axis=1)
        pairs = []
        for s in range(spaces):
            zz, yy, cc = space_coords(s)
            pairs.append((s, space_index((zz + d) % 8, yy, cc)))
        out = out + lax.ppermute(blk, "space", pairs)

    scale = jnp.float32(1.0 / math.sqrt(planes * spaces * NY * NZ))
    return out * scale


def solution(mesh):
    placed = (P("node", "space", None), P("space", None))
    return jax.shard_map(
        per_device, mesh=mesh, in_specs=placed, out_specs=P("node", "space"), check_vma=False
    )
```

```python
import math

import jax
import jax.numpy as jnp
from jax import lax
from jax.experimental import pallas as pl
from jax.experimental.pallas import tpu as pltpu
from jax.sharding import PartitionSpec as P

NY = 128
NZ = 64
ROWS = 32


def ahead(values, offset):
    tail = jnp.zeros(values.shape[:-1] + (offset,), values.dtype)
    return jnp.concatenate([values[..., offset:], tail], axis=-1)


def behind(values, offset):
    head = jnp.zeros(values.shape[:-1] + (offset,), values.dtype)
    return jnp.concatenate([head, values[..., :-offset]], axis=-1)


def stencil_kernel(x_ref, below_ref, above_ref, coef_ref, out_ref):
    span = below_ref.shape[1]
    lane = lax.broadcasted_iota(jnp.int32, (1, span), 1)
    zpos = lane % NZ
    up_ok = zpos != NZ - 1
    down_ok = zpos != 0
    inner = (lane >= NZ) & (lane < span - NZ)
    planes = [x_ref[:, p * span:(p + 1) * span].astype(jnp.float32) for p in range(2)]
    below = below_ref[...].astype(jnp.float32)
    above = above_ref[...].astype(jnp.float32)
    for p in range(2):
        v = planes[p]

        def coef(t):
            return coef_ref[t:t + 1, p * span:(p + 1) * span]

        near = jnp.where(up_ok, pltpu.roll(v, span - 1, 1), 0.0)
        total = coef(0) * (v - near)
        near = jnp.where(down_ok, pltpu.roll(v, 1, 1), 0.0)
        total = total + coef(1) * (v - near)
        total = total + coef(2) * (v - pltpu.roll(v, span - NZ, 1))
        total = total + coef(3) * (v - pltpu.roll(v, NZ, 1))
        total = total + coef(4) * (v - (below if p == 0 else planes[0]))
        total = total + coef(5) * (v - (planes[1] if p == 0 else above))
        out_ref[:, p * span:(p + 1) * span] = jnp.where(inner, total, 0.0).astype(out_ref.dtype)


def stencil(field, below, above, coef):
    snaps, width = field.shape
    span = below.shape[1]
    return pl.pallas_call(
        stencil_kernel,
        grid=(snaps // ROWS,),
        in_specs=[
            pl.BlockSpec((ROWS, width), lambda i: (i, 0)),
            pl.BlockSpec((ROWS, span), lambda i: (i, 0)),
            pl.BlockSpec((ROWS, span), lambda i: (i, 0)),
            pl.BlockSpec(coef.shape, lambda i: (0, 0)),
        ],
        out_specs=pl.BlockSpec((ROWS, width), lambda i: (i, 0)),
        out_shape=jax.ShapeDtypeStruct(field.shape, jnp.bfloat16),
    )(field, below, above, coef)


def weights(kap_chunk, kap_below, kap_above):
    span = kap_chunk.shape[-1]
    kc = kap_chunk.astype(jnp.float32)
    zpos = jnp.arange(span, dtype=jnp.int32) % NZ
    k_zp = jnp.where(zpos != NZ - 1, ahead(kc, 1), 0.0)
    k_zm = jnp.where(zpos != 0, behind(kc, 1), 0.0)
    k_xm = jnp.stack([kap_below.astype(jnp.float32), kc[0]])
    k_xp = jnp.stack([kc[1], kap_above.astype(jnp.float32)])
    near = [k_zp, k_zm, ahead(kc, NZ), behind(kc, NZ), k_xm, k_xp]
    return jnp.stack([0.5 * (kc + k) for k in near]).reshape(6, 2 * span)


def per_device(snapshots, kappa):
    rows, planes, width = snapshots.shape
    nodes = lax.axis_size("node")
    spaces = lax.axis_size("space")
    me = lax.axis_index("node")
    chunk = width // nodes
    span = chunk + 2 * NZ
    snaps = rows * nodes

    up = [(i, i + 1) for i in range(spaces - 1)]
    down = [(j, i) for i, j in up]

    kpad = jnp.pad(kappa, ((0, 0), (NZ, NZ)))
    kap_chunk = lax.dynamic_slice_in_dim(kpad, me * chunk, span, axis=1)
    kap_below = lax.ppermute(kap_chunk[1], "space", up)
    kap_above = lax.ppermute(kap_chunk[0], "space", down)
    coef = weights(kap_chunk, kap_below, kap_above)

    spad = jnp.pad(snapshots, ((0, 0), (0, 0), (NZ, NZ)))
    pieces = jnp.stack([spad[:, :, q * chunk:q * chunk + span] for q in range(nodes)])
    pieces = pieces.reshape(nodes, rows, planes * span)
    field = lax.all_to_all(pieces, "node", 0, 0, tiled=True).reshape(snaps, planes * span)

    below = lax.ppermute(field[:, span:], "space", up)
    above = lax.ppermute(field[:, :span], "space", down)
    image = stencil(field, below, above, coef)
    part = lax.dot_general(image, field, (((1,), (1,)), ((), ())), preferred_element_type=jnp.float32)

    part = part.reshape(nodes, rows, snaps)
    part = lax.all_to_all(part, "node", 0, 0, tiled=True).sum(axis=0)
    part = part.reshape(rows, spaces, snaps // spaces).transpose(1, 0, 2)
    out = lax.all_to_all(part, "space", 0, 0, tiled=True).sum(axis=0)

    scale = jnp.float32(1.0 / math.sqrt(planes * spaces * NY * NZ))
    return out * scale


def solution(mesh):
    placed = (P("node", "space", None), P("space", None))
    return jax.shard_map(
        per_device, mesh=mesh, in_specs=placed, out_specs=P("node", "space"), check_vma=False
    )
```

```python
import math

import jax
import jax.numpy as jnp
from jax import lax
from jax.experimental import pallas as pl
from jax.experimental.pallas import tpu as pltpu
from jax.sharding import PartitionSpec as P

NY = 128
NZ = 64
ROWS = 32
GROUPS = 2


def ahead(values, offset):
    tail = jnp.zeros(values.shape[:-1] + (offset,), values.dtype)
    return jnp.concatenate([values[..., offset:], tail], axis=-1)


def behind(values, offset):
    head = jnp.zeros(values.shape[:-1] + (offset,), values.dtype)
    return jnp.concatenate([head, values[..., :-offset]], axis=-1)


def stencil_kernel(x_ref, below_ref, above_ref, coef_ref, out_ref):
    span = below_ref.shape[1]
    lane = lax.broadcasted_iota(jnp.int32, (1, span), 1)
    zpos = lane % NZ
    up_ok = zpos != NZ - 1
    down_ok = zpos != 0
    inner = lane < span - 2 * NZ
    planes = [x_ref[:, p * span:(p + 1) * span].astype(jnp.float32) for p in range(2)]
    below = below_ref[...].astype(jnp.float32)
    above = above_ref[...].astype(jnp.float32)
    for p in range(2):
        v = planes[p]

        def coef(t):
            return coef_ref[t:t + 1, p * span:(p + 1) * span]

        near = jnp.where(up_ok, pltpu.roll(v, span - 1, 1), 0.0)
        total = coef(0) * (v - near)
        near = jnp.where(down_ok, pltpu.roll(v, 1, 1), 0.0)
        total = total + coef(1) * (v - near)
        total = total + coef(2) * (v - pltpu.roll(v, span - NZ, 1))
        total = total + coef(3) * (v - pltpu.roll(v, NZ, 1))
        total = total + coef(4) * (v - (below if p == 0 else planes[0]))
        total = total + coef(5) * (v - (planes[1] if p == 0 else above))
        out_ref[:, p * span:(p + 1) * span] = jnp.where(inner, total, 0.0).astype(out_ref.dtype)


def stencil(field, below, above, coef):
    snaps, width = field.shape
    span = below.shape[1]
    return pl.pallas_call(
        stencil_kernel,
        grid=(snaps // ROWS,),
        in_specs=[
            pl.BlockSpec((ROWS, width), lambda i: (i, 0)),
            pl.BlockSpec((ROWS, span), lambda i: (i, 0)),
            pl.BlockSpec((ROWS, span), lambda i: (i, 0)),
            pl.BlockSpec(coef.shape, lambda i: (0, 0)),
        ],
        out_specs=pl.BlockSpec((ROWS, width), lambda i: (i, 0)),
        out_shape=jax.ShapeDtypeStruct(field.shape, jnp.bfloat16),
    )(field, below, above, coef)


def weights(kap_chunk, kap_below, kap_above):
    span = kap_chunk.shape[-1]
    kc = kap_chunk.astype(jnp.float32)
    zpos = jnp.arange(span, dtype=jnp.int32) % NZ
    k_zp = jnp.where(zpos != NZ - 1, jnp.roll(kc, -1, axis=-1), 0.0)
    k_zm = jnp.where(zpos != 0, jnp.roll(kc, 1, axis=-1), 0.0)
    k_xm = jnp.stack([kap_below.astype(jnp.float32), kc[0]])
    k_xp = jnp.stack([kc[1], kap_above.astype(jnp.float32)])
    near = [k_zp, k_zm, jnp.roll(kc, -NZ, axis=-1), jnp.roll(kc, NZ, axis=-1), k_xm, k_xp]
    return jnp.stack([0.5 * (kc + k) for k in near]).reshape(6, 2 * span)


def chunked(values, nodes):
    lead = values.shape[:-1]
    cut = values.reshape(lead + (nodes, values.shape[-1] // nodes))
    pad = jnp.zeros(lead + (1, NZ), values.dtype)
    after = jnp.concatenate([cut[..., 1:, :NZ], pad], axis=-2)
    before = jnp.concatenate([pad, cut[..., :-1, -NZ:]], axis=-2)
    pieces = jnp.concatenate([cut, after, before], axis=-1)
    return jnp.moveaxis(pieces, -2, 0)


def per_device(snapshots, kappa):
    rows, planes, width = snapshots.shape
    nodes = lax.axis_size("node")
    spaces = lax.axis_size("space")
    me = lax.axis_index("node")
    chunk = width // nodes
    span = chunk + 2 * NZ
    snaps = rows * nodes

    up = [(i, i + 1) for i in range(spaces - 1)]
    down = [(j, i) for i, j in up]

    kap_chunk = jnp.take(chunked(kappa, nodes), me, axis=0)
    kap_below = lax.ppermute(kap_chunk[1], "space", up)
    kap_above = lax.ppermute(kap_chunk[0], "space", down)
    coef = weights(kap_chunk, kap_below, kap_above)

    pieces = chunked(snapshots, nodes).reshape(nodes, rows, planes * span)
    step = rows // GROUPS
    images, fields = [], []
    for g in range(GROUPS):
        field = lax.all_to_all(pieces[:, g * step:(g + 1) * step], "node", 0, 0, tiled=True)
        field = field.reshape(nodes * step, planes * span)
        below = lax.ppermute(field[:, span:], "space", up)
        above = lax.ppermute(field[:, :span], "space", down)
        images.append(stencil(field, below, above, coef))
        fields.append(field)
    part = jnp.concatenate([
        jnp.concatenate([
            lax.dot_general(im, fd, (((1,), (1,)), ((), ())), preferred_element_type=jnp.float32)
            for fd in fields], axis=1)
        for im in images], axis=0)
    order = (GROUPS, nodes, step)
    part = part.reshape(order + order).transpose(1, 0, 2, 4, 3, 5).reshape(snaps, snaps)

    part = part.reshape(nodes, rows, snaps)
    part = lax.all_to_all(part, "node", 0, 0, tiled=True).sum(axis=0)
    part = part.reshape(rows, spaces, snaps // spaces).transpose(1, 0, 2)
    out = lax.all_to_all(part, "space", 0, 0, tiled=True).sum(axis=0)

    scale = jnp.float32(1.0 / math.sqrt(planes * spaces * NY * NZ))
    return out * scale


def solution(mesh):
    placed = (P("node", "space", None), P("space", None))
    return jax.shard_map(
        per_device, mesh=mesh, in_specs=placed, out_specs=P("node", "space"), check_vma=False
    )
```

```python
import math

import jax
import jax.numpy as jnp
from jax import lax
from jax.experimental import pallas as pl
from jax.experimental.pallas import tpu as pltpu
from jax.sharding import PartitionSpec as P

NY = 128
NZ = 64
ROWS = 32
GROUPS = 2


def ahead(values, offset):
    tail = jnp.zeros(values.shape[:-1] + (offset,), values.dtype)
    return jnp.concatenate([values[..., offset:], tail], axis=-1)


def behind(values, offset):
    head = jnp.zeros(values.shape[:-1] + (offset,), values.dtype)
    return jnp.concatenate([head, values[..., :-offset]], axis=-1)


def stencil_kernel(x_ref, below_ref, above_ref, coef_ref, out_ref):
    span = below_ref.shape[1]
    lane = lax.broadcasted_iota(jnp.int32, (1, span), 1)
    zpos = lane % NZ
    up_ok = zpos != NZ - 1
    down_ok = zpos != 0
    inner = lane < span - 2 * NZ
    planes = [x_ref[p].astype(jnp.float32) for p in range(2)]
    below = below_ref[...].astype(jnp.float32)
    above = above_ref[...].astype(jnp.float32)
    for p in range(2):
        v = planes[p]

        def coef(t):
            return coef_ref[t, p:p + 1, :]

        near = jnp.where(up_ok, pltpu.roll(v, span - 1, 1), 0.0)
        total = coef(0) * (v - near)
        near = jnp.where(down_ok, pltpu.roll(v, 1, 1), 0.0)
        total = total + coef(1) * (v - near)
        total = total + coef(2) * (v - pltpu.roll(v, span - NZ, 1))
        total = total + coef(3) * (v - pltpu.roll(v, NZ, 1))
        total = total + coef(4) * (v - (below if p == 0 else planes[0]))
        total = total + coef(5) * (v - (planes[1] if p == 0 else above))
        out_ref[p] = jnp.where(inner, total, 0.0).astype(out_ref.dtype)


def stencil(field, below, above, coef):
    planes, snaps, span = field.shape
    return pl.pallas_call(
        stencil_kernel,
        grid=(snaps // ROWS,),
        in_specs=[
            pl.BlockSpec((planes, ROWS, span), lambda i: (0, i, 0)),
            pl.BlockSpec((ROWS, span), lambda i: (i, 0)),
            pl.BlockSpec((ROWS, span), lambda i: (i, 0)),
            pl.BlockSpec(coef.shape, lambda i: (0, 0, 0)),
        ],
        out_specs=pl.BlockSpec((planes, ROWS, span), lambda i: (0, i, 0)),
        out_shape=jax.ShapeDtypeStruct(field.shape, jnp.bfloat16),
    )(field, below, above, coef)


def weights(kap_chunk, kap_below, kap_above):
    span = kap_chunk.shape[-1]
    kc = kap_chunk.astype(jnp.float32)
    zpos = jnp.arange(span, dtype=jnp.int32) % NZ
    k_zp = jnp.where(zpos != NZ - 1, jnp.roll(kc, -1, axis=-1), 0.0)
    k_zm = jnp.where(zpos != 0, jnp.roll(kc, 1, axis=-1), 0.0)
    k_xm = jnp.stack([kap_below.astype(jnp.float32), kc[0]])
    k_xp = jnp.stack([kc[1], kap_above.astype(jnp.float32)])
    near = [k_zp, k_zm, jnp.roll(kc, -NZ, axis=-1), jnp.roll(kc, NZ, axis=-1), k_xm, k_xp]
    return jnp.stack([0.5 * (kc + k) for k in near])


def chunked(values, nodes):
    chunk = values.shape[-1] // nodes
    zero = jnp.zeros(values.shape[:-1] + (NZ,), values.dtype)
    pieces = []
    for q in range(nodes):
        after = values[..., (q + 1) * chunk:(q + 1) * chunk + NZ] if q + 1 < nodes else zero
        before = values[..., q * chunk - NZ:q * chunk] if q > 0 else zero
        pieces.append(jnp.concatenate([values[..., q * chunk:(q + 1) * chunk], after, before], axis=-1))
    return jnp.stack(pieces, axis=-3)


def per_device(snapshots, kappa):
    rows, planes, width = snapshots.shape
    nodes = lax.axis_size("node")
    spaces = lax.axis_size("space")
    me = lax.axis_index("node")
    chunk = width // nodes
    span = chunk + 2 * NZ
    snaps = rows * nodes

    up = [(i, i + 1) for i in range(spaces - 1)]
    down = [(j, i) for i, j in up]

    kap_chunk = jnp.take(chunked(kappa[:, None], nodes)[:, :, 0], me, axis=1)
    kap_below = lax.ppermute(kap_chunk[1], "space", up)
    kap_above = lax.ppermute(kap_chunk[0], "space", down)
    coef = weights(kap_chunk, kap_below, kap_above)

    major = jnp.transpose(snapshots, (1, 0, 2))
    step = rows // GROUPS
    images, fields = [], []
    for g in range(GROUPS):
        pieces = chunked(major[:, g * step:(g + 1) * step], nodes)
        field = lax.all_to_all(pieces, "node", 1, 1, tiled=True).reshape(planes, nodes * step, span)
        below = lax.ppermute(field[1], "space", up)
        above = lax.ppermute(field[0], "space", down)
        images.append(stencil(field, below, above, coef))
        fields.append(field)
    dims = (((0, 2), (0, 2)), ((), ()))
    part = jnp.concatenate([
        jnp.concatenate([
            lax.dot_general(im, fd, dims, preferred_element_type=jnp.float32)
            for fd in fields], axis=1)
        for im in images], axis=0)
    order = (GROUPS, nodes, step)
    part = part.reshape(order + order).transpose(1, 0, 2, 4, 3, 5).reshape(snaps, snaps)

    part = part.reshape(nodes, rows, snaps)
    part = lax.all_to_all(part, "node", 0, 0, tiled=True).sum(axis=0)
    part = part.reshape(rows, spaces, snaps // spaces).transpose(1, 0, 2)
    out = lax.all_to_all(part, "space", 0, 0, tiled=True).sum(axis=0)

    scale = jnp.float32(1.0 / math.sqrt(planes * spaces * NY * NZ))
    return out * scale


def solution(mesh):
    placed = (P("node", "space", None), P("space", None))
    return jax.shard_map(
        per_device, mesh=mesh, in_specs=placed, out_specs=P("node", "space"), check_vma=False
    )
```

```python
import math

import jax
import jax.numpy as jnp
from jax import lax
from jax.experimental import pallas as pl
from jax.experimental.pallas import tpu as pltpu
from jax.sharding import Mesh, PartitionSpec as P

NY = 128
NZ = 64
ROWS = 32
GROUPS = 2
SPACE = ("z", "y", "core")


def ahead(values, offset):
    tail = jnp.zeros(values.shape[:-1] + (offset,), values.dtype)
    return jnp.concatenate([values[..., offset:], tail], axis=-1)


def behind(values, offset):
    head = jnp.zeros(values.shape[:-1] + (offset,), values.dtype)
    return jnp.concatenate([head, values[..., :-offset]], axis=-1)


def stencil_kernel(x_ref, below_ref, above_ref, coef_ref, out_ref):
    span = below_ref.shape[1]
    lane = lax.broadcasted_iota(jnp.int32, (1, span), 1)
    zpos = lane % NZ
    up_ok = zpos != NZ - 1
    down_ok = zpos != 0
    inner = lane < span - 2 * NZ
    planes = [x_ref[p].astype(jnp.float32) for p in range(2)]
    below = below_ref[...].astype(jnp.float32)
    above = above_ref[...].astype(jnp.float32)
    for p in range(2):
        v = planes[p]

        def coef(t):
            return coef_ref[t, p:p + 1, :]

        near = jnp.where(up_ok, pltpu.roll(v, span - 1, 1), 0.0)
        total = coef(0) * (v - near)
        near = jnp.where(down_ok, pltpu.roll(v, 1, 1), 0.0)
        total = total + coef(1) * (v - near)
        total = total + coef(2) * (v - pltpu.roll(v, span - NZ, 1))
        total = total + coef(3) * (v - pltpu.roll(v, NZ, 1))
        total = total + coef(4) * (v - (below if p == 0 else planes[0]))
        total = total + coef(5) * (v - (planes[1] if p == 0 else above))
        out_ref[p] = jnp.where(inner, total, 0.0).astype(out_ref.dtype)


def stencil(field, below, above, coef):
    planes, snaps, span = field.shape
    return pl.pallas_call(
        stencil_kernel,
        grid=(snaps // ROWS,),
        in_specs=[
            pl.BlockSpec((planes, ROWS, span), lambda i: (0, i, 0)),
            pl.BlockSpec((ROWS, span), lambda i: (i, 0)),
            pl.BlockSpec((ROWS, span), lambda i: (i, 0)),
            pl.BlockSpec(coef.shape, lambda i: (0, 0, 0)),
        ],
        out_specs=pl.BlockSpec((planes, ROWS, span), lambda i: (0, i, 0)),
        out_shape=jax.ShapeDtypeStruct(field.shape, jnp.bfloat16),
    )(field, below, above, coef)


def weights(kap_chunk, kap_below, kap_above):
    span = kap_chunk.shape[-1]
    kc = kap_chunk.astype(jnp.float32)
    zpos = jnp.arange(span, dtype=jnp.int32) % NZ
    k_zp = jnp.where(zpos != NZ - 1, jnp.roll(kc, -1, axis=-1), 0.0)
    k_zm = jnp.where(zpos != 0, jnp.roll(kc, 1, axis=-1), 0.0)
    k_xm = jnp.stack([kap_below.astype(jnp.float32), kc[0]])
    k_xp = jnp.stack([kc[1], kap_above.astype(jnp.float32)])
    near = [k_zp, k_zm, jnp.roll(kc, -NZ, axis=-1), jnp.roll(kc, NZ, axis=-1), k_xm, k_xp]
    return jnp.stack([0.5 * (kc + k) for k in near])


def chunked(values, nodes):
    chunk = values.shape[-1] // nodes
    zero = jnp.zeros(values.shape[:-1] + (NZ,), values.dtype)
    pieces = []
    for q in range(nodes):
        after = values[..., (q + 1) * chunk:(q + 1) * chunk + NZ] if q + 1 < nodes else zero
        before = values[..., q * chunk - NZ:q * chunk] if q > 0 else zero
        pieces.append(jnp.concatenate([values[..., q * chunk:(q + 1) * chunk], after, before], axis=-1))
    return jnp.stack(pieces, axis=-3)


def per_device(snapshots, kappa):
    rows, planes, width = snapshots.shape
    nodes = lax.axis_size("node")
    sizes = [lax.axis_size(a) for a in SPACE]
    spaces = math.prod(sizes)
    me = lax.axis_index("node")
    chunk = width // nodes
    span = chunk + 2 * NZ
    snaps = rows * nodes

    up = [(i, i + 1) for i in range(spaces - 1)]
    down = [(j, i) for i, j in up]

    kap_chunk = jnp.take(chunked(kappa[:, None], nodes)[:, :, 0], me, axis=1)
    kap_below = lax.ppermute(kap_chunk[1], SPACE, up)
    kap_above = lax.ppermute(kap_chunk[0], SPACE, down)
    coef = weights(kap_chunk, kap_below, kap_above)

    major = jnp.transpose(snapshots, (1, 0, 2))
    step = rows // GROUPS
    images, fields = [], []
    for g in range(GROUPS):
        pieces = chunked(major[:, g * step:(g + 1) * step], nodes)
        field = lax.all_to_all(pieces, "node", 1, 1, tiled=True).reshape(planes, nodes * step, span)
        below = lax.ppermute(field[1], SPACE, up)
        above = lax.ppermute(field[0], SPACE, down)
        images.append(stencil(field, below, above, coef))
        fields.append(field)
    dims = (((0, 2), (0, 2)), ((), ()))
    part = jnp.concatenate([
        jnp.concatenate([
            lax.dot_general(im, fd, dims, preferred_element_type=jnp.float32)
            for fd in fields], axis=1)
        for im in images], axis=0)
    part = part.reshape(GROUPS, nodes, step, snaps)
    total = jnp.take(part, me, axis=1)
    for d in range(1, nodes):
        blk = jnp.take(part, (me + d) % nodes, axis=1)
        total = total + lax.ppermute(blk, "node", [(i, (i + d) % nodes) for i in range(nodes)])
    total = total.reshape(rows, GROUPS, nodes, step).transpose(0, 2, 1, 3)
    total = total.reshape((rows,) + tuple(sizes) + (snaps // spaces,))
    for axis in reversed(range(len(SPACE))):
        total = jnp.moveaxis(total, axis + 1, 0)
        total = lax.all_to_all(total, SPACE[axis], 0, 0, tiled=True).sum(axis=0)
    out = total

    scale = jnp.float32(1.0 / math.sqrt(planes * spaces * NY * NZ))
    return out * scale


def solution(mesh):
    node, space = mesh.devices.shape
    cores = 2
    fine = Mesh(mesh.devices.reshape(node, space // (4 * cores), 4, cores), ("node",) + SPACE)
    placed = (P("node", SPACE, None), P(SPACE, None))
    return jax.shard_map(
        per_device, mesh=fine, in_specs=placed, out_specs=P("node", SPACE), check_vma=False
    )
```

```python
import math

import jax
import jax.numpy as jnp
from jax import lax
from jax.experimental import pallas as pl
from jax.experimental.pallas import tpu as pltpu
from jax.sharding import Mesh, PartitionSpec as P

NY = 128
NZ = 64
ROWS = 32
GROUPS = 2
SPACE = ("z", "y", "core")


def ahead(values, offset):
    tail = jnp.zeros(values.shape[:-1] + (offset,), values.dtype)
    return jnp.concatenate([values[..., offset:], tail], axis=-1)


def behind(values, offset):
    head = jnp.zeros(values.shape[:-1] + (offset,), values.dtype)
    return jnp.concatenate([head, values[..., :-offset]], axis=-1)


def stencil_kernel(x_ref, below_ref, above_ref, coef_ref, out_ref):
    span = below_ref.shape[1]
    lane = lax.broadcasted_iota(jnp.int32, (1, span), 1)
    zpos = lane % NZ
    up_ok = zpos != NZ - 1
    down_ok = zpos != 0
    inner = lane < span - 2 * NZ
    planes = [x_ref[p].astype(jnp.float32) for p in range(2)]
    below = below_ref[...].astype(jnp.float32)
    above = above_ref[...].astype(jnp.float32)
    for p in range(2):
        v = planes[p]

        def coef(t):
            return coef_ref[t, p:p + 1, :]

        near = jnp.where(up_ok, pltpu.roll(v, span - 1, 1), 0.0)
        total = coef(0) * (v - near)
        near = jnp.where(down_ok, pltpu.roll(v, 1, 1), 0.0)
        total = total + coef(1) * (v - near)
        total = total + coef(2) * (v - pltpu.roll(v, span - NZ, 1))
        total = total + coef(3) * (v - pltpu.roll(v, NZ, 1))
        total = total + coef(4) * (v - (below if p == 0 else planes[0]))
        total = total + coef(5) * (v - (planes[1] if p == 0 else above))
        out_ref[p] = jnp.where(inner, total, 0.0).astype(out_ref.dtype)


def stencil(field, below, above, coef):
    planes, snaps, span = field.shape
    return pl.pallas_call(
        stencil_kernel,
        grid=(snaps // ROWS,),
        in_specs=[
            pl.BlockSpec((planes, ROWS, span), lambda i: (0, i, 0)),
            pl.BlockSpec((ROWS, span), lambda i: (i, 0)),
            pl.BlockSpec((ROWS, span), lambda i: (i, 0)),
            pl.BlockSpec(coef.shape, lambda i: (0, 0, 0)),
        ],
        out_specs=pl.BlockSpec((planes, ROWS, span), lambda i: (0, i, 0)),
        out_shape=jax.ShapeDtypeStruct(field.shape, jnp.bfloat16),
    )(field, below, above, coef)


def weights(kap_chunk, kap_below, kap_above):
    span = kap_chunk.shape[-1]
    kc = kap_chunk.astype(jnp.float32)
    zpos = jnp.arange(span, dtype=jnp.int32) % NZ
    k_zp = jnp.where(zpos != NZ - 1, jnp.roll(kc, -1, axis=-1), 0.0)
    k_zm = jnp.where(zpos != 0, jnp.roll(kc, 1, axis=-1), 0.0)
    k_xm = jnp.stack([kap_below.astype(jnp.float32), kc[0]])
    k_xp = jnp.stack([kc[1], kap_above.astype(jnp.float32)])
    near = [k_zp, k_zm, jnp.roll(kc, -NZ, axis=-1), jnp.roll(kc, NZ, axis=-1), k_xm, k_xp]
    return jnp.stack([0.5 * (kc + k) for k in near])


def chunked(values, nodes):
    chunk = values.shape[-1] // nodes
    zero = jnp.zeros(values.shape[:-1] + (NZ,), values.dtype)
    pieces = []
    for q in range(nodes):
        after = values[..., (q + 1) * chunk:(q + 1) * chunk + NZ] if q + 1 < nodes else zero
        before = values[..., q * chunk - NZ:q * chunk] if q > 0 else zero
        pieces.append(jnp.concatenate([values[..., q * chunk:(q + 1) * chunk], after, before], axis=-1))
    return jnp.stack(pieces, axis=-3)


def per_device(snapshots, kappa):
    rows, planes, width = snapshots.shape
    nodes = lax.axis_size("node")
    sizes = [lax.axis_size(a) for a in SPACE]
    spaces = math.prod(sizes)
    me = lax.axis_index("node")
    chunk = width // nodes
    span = chunk + 2 * NZ
    snaps = rows * nodes

    up = [(i, i + 1) for i in range(spaces - 1)]
    down = [(j, i) for i, j in up]

    kap_chunk = jnp.take(chunked(kappa[:, None], nodes)[:, :, 0], me, axis=1)
    kap_below = lax.ppermute(kap_chunk[1], SPACE, up)
    kap_above = lax.ppermute(kap_chunk[0], SPACE, down)
    coef = weights(kap_chunk, kap_below, kap_above)

    major = jnp.transpose(snapshots, (1, 0, 2))
    step = rows // GROUPS
    images, fields = [], []
    for g in range(GROUPS):
        pieces = chunked(major[:, g * step:(g + 1) * step], nodes)
        field = lax.all_to_all(pieces, "node", 1, 1, tiled=True).reshape(planes, nodes * step, span)
        below = lax.ppermute(field[1], SPACE, up)
        above = lax.ppermute(field[0], SPACE, down)
        images.append(stencil(field, below, above, coef))
        fields.append(field)
    dims = (((0, 2), (0, 2)), ((), ()))
    part = jnp.concatenate([
        jnp.concatenate([
            lax.dot_general(im, fd, dims, preferred_element_type=jnp.float32)
            for fd in fields], axis=1)
        for im in images], axis=0)
    cols = (GROUPS, nodes, sizes[0] // (GROUPS * nodes), sizes[1], sizes[2], snaps // spaces)
    part = part.reshape((snaps,) + cols)
    part = jnp.moveaxis(part, 5, 0)
    part = lax.all_to_all(part, SPACE[2], 0, 0, tiled=True).sum(axis=0)
    part = part.reshape(GROUPS, nodes, step, -1)
    total = jnp.take(part, me, axis=1)
    for d in range(1, nodes):
        blk = jnp.take(part, (me + d) % nodes, axis=1)
        total = total + lax.ppermute(blk, "node", [(i, (i + d) % nodes) for i in range(nodes)])
    total = total.reshape((rows,) + cols[:4] + cols[5:])
    total = total.transpose(0, 2, 1, 3, 4, 5)
    total = total.reshape((rows,) + tuple(sizes[:2]) + (snaps // spaces,))
    for axis in (1, 0):
        total = jnp.moveaxis(total, axis + 1, 0)
        total = lax.all_to_all(total, SPACE[axis], 0, 0, tiled=True).sum(axis=0)
    out = total

    scale = jnp.float32(1.0 / math.sqrt(planes * spaces * NY * NZ))
    return out * scale


def solution(mesh):
    node, space = mesh.devices.shape
    cores = 2
    fine = Mesh(mesh.devices.reshape(node, space // (4 * cores), 4, cores), ("node",) + SPACE)
    placed = (P("node", SPACE, None), P(SPACE, None))
    return jax.shard_map(
        per_device, mesh=fine, in_specs=placed, out_specs=P("node", SPACE), check_vma=False
    )
```

```python
import math

import jax
import jax.numpy as jnp
from jax import lax
from jax.experimental import pallas as pl
from jax.experimental.pallas import tpu as pltpu
from jax.sharding import Mesh, PartitionSpec as P

NY = 128
NZ = 64
ROWS = 32
GROUPS = 2
SPACE = ("z", "y", "core")


def ahead(values, offset):
    tail = jnp.zeros(values.shape[:-1] + (offset,), values.dtype)
    return jnp.concatenate([values[..., offset:], tail], axis=-1)


def behind(values, offset):
    head = jnp.zeros(values.shape[:-1] + (offset,), values.dtype)
    return jnp.concatenate([head, values[..., :-offset]], axis=-1)


def stencil_kernel(x_ref, below_ref, above_ref, coef_ref, out_ref):
    span = below_ref.shape[1]
    lane = lax.broadcasted_iota(jnp.int32, (1, span), 1)
    zpos = lane % NZ
    up_ok = zpos != NZ - 1
    down_ok = zpos != 0
    inner = lane < span - 2 * NZ
    planes = [x_ref[p].astype(jnp.float32) for p in range(2)]
    below = below_ref[...].astype(jnp.float32)
    above = above_ref[...].astype(jnp.float32)
    for p in range(2):
        v = planes[p]

        def coef(t):
            return coef_ref[t, p:p + 1, :]

        near = jnp.where(up_ok, pltpu.roll(v, span - 1, 1), 0.0)
        total = coef(0) * (v - near)
        near = jnp.where(down_ok, pltpu.roll(v, 1, 1), 0.0)
        total = total + coef(1) * (v - near)
        total = total + coef(2) * (v - pltpu.roll(v, span - NZ, 1))
        total = total + coef(3) * (v - pltpu.roll(v, NZ, 1))
        total = total + coef(4) * (v - (below if p == 0 else planes[0]))
        total = total + coef(5) * (v - (planes[1] if p == 0 else above))
        out_ref[p] = jnp.where(inner, total, 0.0).astype(out_ref.dtype)


def stencil(field, below, above, coef):
    planes, snaps, span = field.shape
    return pl.pallas_call(
        stencil_kernel,
        grid=(snaps // ROWS,),
        in_specs=[
            pl.BlockSpec((planes, ROWS, span), lambda i: (0, i, 0)),
            pl.BlockSpec((ROWS, span), lambda i: (i, 0)),
            pl.BlockSpec((ROWS, span), lambda i: (i, 0)),
            pl.BlockSpec(coef.shape, lambda i: (0, 0, 0)),
        ],
        out_specs=pl.BlockSpec((planes, ROWS, span), lambda i: (0, i, 0)),
        out_shape=jax.ShapeDtypeStruct(field.shape, jnp.bfloat16),
    )(field, below, above, coef)


def weights(kap_chunk, kap_below, kap_above):
    span = kap_chunk.shape[-1]
    kc = kap_chunk.astype(jnp.float32)
    zpos = jnp.arange(span, dtype=jnp.int32) % NZ
    k_zp = jnp.where(zpos != NZ - 1, jnp.roll(kc, -1, axis=-1), 0.0)
    k_zm = jnp.where(zpos != 0, jnp.roll(kc, 1, axis=-1), 0.0)
    k_xm = jnp.stack([kap_below.astype(jnp.float32), kc[0]])
    k_xp = jnp.stack([kc[1], kap_above.astype(jnp.float32)])
    near = [k_zp, k_zm, jnp.roll(kc, -NZ, axis=-1), jnp.roll(kc, NZ, axis=-1), k_xm, k_xp]
    return jnp.stack([0.5 * (kc + k) for k in near])


def chunked(values, nodes):
    chunk = values.shape[-1] // nodes
    zero = jnp.zeros(values.shape[:-1] + (NZ,), values.dtype)
    pieces = []
    for q in range(nodes):
        after = values[..., (q + 1) * chunk:(q + 1) * chunk + NZ] if q + 1 < nodes else zero
        before = values[..., q * chunk - NZ:q * chunk] if q > 0 else zero
        pieces.append(jnp.concatenate([values[..., q * chunk:(q + 1) * chunk], after, before], axis=-1))
    return jnp.stack(pieces, axis=-3)


def per_device(snapshots, kappa):
    rows, planes, width = snapshots.shape
    nodes = lax.axis_size("node")
    sizes = [lax.axis_size(a) for a in SPACE]
    spaces = math.prod(sizes)
    me = lax.axis_index("node")
    chunk = width // nodes
    span = chunk + 2 * NZ
    snaps = rows * nodes

    up = [(i, i + 1) for i in range(spaces - 1)]
    down = [(j, i) for i, j in up]

    kap_chunk = jnp.take(chunked(kappa[:, None], nodes)[:, :, 0], me, axis=1)
    kap_below = lax.ppermute(kap_chunk[1], SPACE, up)
    kap_above = lax.ppermute(kap_chunk[0], SPACE, down)
    coef = weights(kap_chunk, kap_below, kap_above)

    major = jnp.transpose(snapshots, (1, 0, 2))
    step = rows // GROUPS
    images, fields = [], []
    for g in range(GROUPS):
        pieces = chunked(major[:, g * step:(g + 1) * step], nodes)
        field = lax.all_to_all(pieces, "node", 1, 1, tiled=True).reshape(planes, nodes * step, span)
        below = lax.ppermute(field[1], SPACE, up)
        above = lax.ppermute(field[0], SPACE, down)
        images.append(stencil(field, below, above, coef))
        fields.append(field)
    dims = (((0, 2), (0, 2)), ((), ()))
    part = jnp.concatenate([
        jnp.concatenate([
            lax.dot_general(im, fd, dims, preferred_element_type=jnp.float32)
            for fd in fields], axis=1)
        for im in images], axis=0)
    width = snaps // spaces
    part = part.reshape(GROUPS, nodes, step, GROUPS, nodes, step // width, width)
    part = part.transpose(1, 4, 3, 5, 0, 2, 6).reshape(nodes * spaces, rows, width)
    total = lax.all_to_all(part, ("node",) + SPACE, 0, 0, tiled=True).sum(axis=0)
    out = total

    scale = jnp.float32(1.0 / math.sqrt(planes * spaces * NY * NZ))
    return out * scale


def solution(mesh):
    node, space = mesh.devices.shape
    cores = 2
    fine = Mesh(mesh.devices.reshape(node, space // (4 * cores), 4, cores), ("node",) + SPACE)
    placed = (P("node", SPACE, None), P(SPACE, None))
    return jax.shard_map(
        per_device, mesh=fine, in_specs=placed, out_specs=P("node", SPACE), check_vma=False
    )
```

```python
import math

import jax
import jax.numpy as jnp
from jax import lax
from jax.experimental import pallas as pl
from jax.experimental.pallas import tpu as pltpu
from jax.sharding import Mesh, PartitionSpec as P

NY = 128
NZ = 64
ROWS = 32
GROUPS = 2
SPACE = ("z", "y", "core")


def ahead(values, offset):
    tail = jnp.zeros(values.shape[:-1] + (offset,), values.dtype)
    return jnp.concatenate([values[..., offset:], tail], axis=-1)


def behind(values, offset):
    head = jnp.zeros(values.shape[:-1] + (offset,), values.dtype)
    return jnp.concatenate([head, values[..., :-offset]], axis=-1)


def stencil_kernel(x_ref, below_ref, above_ref, coef_ref, out_ref):
    span = below_ref.shape[1]
    lane = lax.broadcasted_iota(jnp.int32, (1, span), 1)
    zpos = lane % NZ
    up_ok = zpos != NZ - 1
    down_ok = zpos != 0
    inner = lane < span - 2 * NZ
    planes = [x_ref[p].astype(jnp.float32) for p in range(2)]
    below = below_ref[...].astype(jnp.float32)
    above = above_ref[...].astype(jnp.float32)
    for p in range(2):
        v = planes[p]

        def coef(t):
            return coef_ref[t, p:p + 1, :]

        near = jnp.where(up_ok, pltpu.roll(v, span - 1, 1), 0.0)
        total = coef(0) * (v - near)
        near = jnp.where(down_ok, pltpu.roll(v, 1, 1), 0.0)
        total = total + coef(1) * (v - near)
        total = total + coef(2) * (v - pltpu.roll(v, span - NZ, 1))
        total = total + coef(3) * (v - pltpu.roll(v, NZ, 1))
        total = total + coef(4) * (v - (below if p == 0 else planes[0]))
        total = total + coef(5) * (v - (planes[1] if p == 0 else above))
        out_ref[p] = jnp.where(inner, total, 0.0).astype(out_ref.dtype)


def stencil(field, below, above, coef):
    planes, snaps, span = field.shape
    return pl.pallas_call(
        stencil_kernel,
        grid=(snaps // ROWS,),
        in_specs=[
            pl.BlockSpec((planes, ROWS, span), lambda i: (0, i, 0)),
            pl.BlockSpec((ROWS, span), lambda i: (i, 0)),
            pl.BlockSpec((ROWS, span), lambda i: (i, 0)),
            pl.BlockSpec(coef.shape, lambda i: (0, 0, 0)),
        ],
        out_specs=pl.BlockSpec((planes, ROWS, span), lambda i: (0, i, 0)),
        out_shape=jax.ShapeDtypeStruct(field.shape, jnp.bfloat16),
    )(field, below, above, coef)


def weights(kap_chunk, kap_below, kap_above):
    span = kap_chunk.shape[-1]
    kc = kap_chunk.astype(jnp.float32)
    zpos = jnp.arange(span, dtype=jnp.int32) % NZ
    k_zp = jnp.where(zpos != NZ - 1, jnp.roll(kc, -1, axis=-1), 0.0)
    k_zm = jnp.where(zpos != 0, jnp.roll(kc, 1, axis=-1), 0.0)
    k_xm = jnp.stack([kap_below.astype(jnp.float32), kc[0]])
    k_xp = jnp.stack([kc[1], kap_above.astype(jnp.float32)])
    near = [k_zp, k_zm, jnp.roll(kc, -NZ, axis=-1), jnp.roll(kc, NZ, axis=-1), k_xm, k_xp]
    return jnp.stack([0.5 * (kc + k) for k in near])


def chunked(values, nodes):
    chunk = values.shape[-1] // nodes
    zero = jnp.zeros(values.shape[:-1] + (NZ,), values.dtype)
    pieces = []
    for q in range(nodes):
        after = values[..., (q + 1) * chunk:(q + 1) * chunk + NZ] if q + 1 < nodes else zero
        before = values[..., q * chunk - NZ:q * chunk] if q > 0 else zero
        pieces.append(jnp.concatenate([values[..., q * chunk:(q + 1) * chunk], after, before], axis=-1))
    return jnp.stack(pieces, axis=-3)


def exchanged(pieces, me, nodes):
    def shift(value, by):
        return lax.ppermute(value, "node", [(i, (i + by) % nodes) for i in range(nodes)])

    half = pieces.shape[2] // 2
    far = jnp.take(pieces, (me + 2) % nodes, axis=1)
    leg_up = shift(far[:, :half], 1)
    leg_down = shift(far[:, half:], -1)
    from_below = shift(jnp.take(pieces, (me + 1) % nodes, axis=1), 1)
    from_above = shift(jnp.take(pieces, (me - 1) % nodes, axis=1), -1)
    far = jnp.concatenate([shift(leg_up, 1), shift(leg_down, -1)], axis=1)
    return jnp.stack([jnp.take(pieces, me, axis=1), from_below, far, from_above], axis=1)


def per_device(snapshots, kappa):
    rows, planes, width = snapshots.shape
    nodes = lax.axis_size("node")
    sizes = [lax.axis_size(a) for a in SPACE]
    spaces = math.prod(sizes)
    me = lax.axis_index("node")
    chunk = width // nodes
    span = chunk + 2 * NZ
    snaps = rows * nodes

    up = [(i, i + 1) for i in range(spaces - 1)]
    down = [(j, i) for i, j in up]

    kap_chunk = jnp.take(chunked(kappa[:, None], nodes)[:, :, 0], me, axis=1)
    kap_below = lax.ppermute(kap_chunk[1], SPACE, up)
    kap_above = lax.ppermute(kap_chunk[0], SPACE, down)
    coef = weights(kap_chunk, kap_below, kap_above)

    major = jnp.transpose(snapshots, (1, 0, 2))
    step = rows // GROUPS
    images, fields = [], []
    for g in range(GROUPS):
        pieces = chunked(major[:, g * step:(g + 1) * step], nodes)
        field = exchanged(pieces, me, nodes).reshape(planes, nodes * step, span)
        below = lax.ppermute(field[1], SPACE, up)
        above = lax.ppermute(field[0], SPACE, down)
        images.append(stencil(field, below, above, coef))
        fields.append(field)
    dims = (((0, 2), (0, 2)), ((), ()))
    part = jnp.concatenate([
        jnp.concatenate([
            lax.dot_general(im, fd, dims, preferred_element_type=jnp.float32)
            for fd in fields], axis=1)
        for im in images], axis=0)
    part = part.reshape(GROUPS, nodes, step, GROUPS, nodes, step)
    part = jnp.take(part, (me - jnp.arange(nodes)) % nodes, axis=4).reshape(GROUPS, nodes, step, snaps)
    total = part[:, 0]
    for d in range(1, nodes):
        blk = part[:, (nodes - d) % nodes]
        total = total + lax.ppermute(blk, "node", [(i, (i + d) % nodes) for i in range(nodes)])
    total = total.reshape(rows, GROUPS, nodes, step).transpose(0, 2, 1, 3)
    total = total.reshape((rows,) + tuple(sizes) + (snaps // spaces,))
    for axis in reversed(range(len(SPACE))):
        total = jnp.moveaxis(total, axis + 1, 0)
        total = lax.all_to_all(total, SPACE[axis], 0, 0, tiled=True).sum(axis=0)
    out = total

    scale = jnp.float32(1.0 / math.sqrt(planes * spaces * NY * NZ))
    return out * scale


def solution(mesh):
    node, space = mesh.devices.shape
    cores = 2
    fine = Mesh(mesh.devices.reshape(node, space // (4 * cores), 4, cores), ("node",) + SPACE)
    placed = (P("node", SPACE, None), P(SPACE, None))
    return jax.shard_map(
        per_device, mesh=fine, in_specs=placed, out_specs=P("node", SPACE), check_vma=False
    )
```

```python
import math

import jax
import jax.numpy as jnp
from jax import lax
from jax.experimental import pallas as pl
from jax.experimental.pallas import tpu as pltpu
from jax.sharding import Mesh, PartitionSpec as P

NY = 128
NZ = 64
ROWS = 32
GROUPS = 2
SPACE = ("z", "y", "core")


def ahead(values, offset):
    tail = jnp.zeros(values.shape[:-1] + (offset,), values.dtype)
    return jnp.concatenate([values[..., offset:], tail], axis=-1)


def behind(values, offset):
    head = jnp.zeros(values.shape[:-1] + (offset,), values.dtype)
    return jnp.concatenate([head, values[..., :-offset]], axis=-1)


def stencil_kernel(x_ref, below_ref, above_ref, coef_ref, out_ref):
    span = below_ref.shape[1]
    lane = lax.broadcasted_iota(jnp.int32, (1, span), 1)
    inner = lane < span - 2 * NZ
    planes = [x_ref[p].astype(jnp.float32) for p in range(2)]
    below = below_ref[...].astype(jnp.float32)
    above = above_ref[...].astype(jnp.float32)
    for p in range(2):
        v = planes[p]

        def coef(t):
            return coef_ref[t, p:p + 1, :]

        near = coef(0) * pltpu.roll(v, span - 1, 1)
        near = near + coef(1) * pltpu.roll(v, 1, 1)
        near = near + coef(2) * pltpu.roll(v, span - NZ, 1)
        near = near + coef(3) * pltpu.roll(v, NZ, 1)
        near = near + coef(4) * (below if p == 0 else planes[0])
        near = near + coef(5) * (planes[1] if p == 0 else above)
        total = coef(6) * v - near
        out_ref[p] = jnp.where(inner, total, 0.0).astype(out_ref.dtype)


def stencil(field, below, above, coef):
    planes, snaps, span = field.shape
    return pl.pallas_call(
        stencil_kernel,
        grid=(snaps // ROWS,),
        in_specs=[
            pl.BlockSpec((planes, ROWS, span), lambda i: (0, i, 0)),
            pl.BlockSpec((ROWS, span), lambda i: (i, 0)),
            pl.BlockSpec((ROWS, span), lambda i: (i, 0)),
            pl.BlockSpec(coef.shape, lambda i: (0, 0, 0)),
        ],
        out_specs=pl.BlockSpec((planes, ROWS, span), lambda i: (0, i, 0)),
        out_shape=jax.ShapeDtypeStruct(field.shape, jnp.bfloat16),
    )(field, below, above, coef)


def weights(kap_chunk, kap_below, kap_above):
    span = kap_chunk.shape[-1]
    kc = kap_chunk.astype(jnp.float32)
    zpos = jnp.arange(span, dtype=jnp.int32) % NZ
    k_zp = jnp.where(zpos != NZ - 1, jnp.roll(kc, -1, axis=-1), 0.0)
    k_zm = jnp.where(zpos != 0, jnp.roll(kc, 1, axis=-1), 0.0)
    k_xm = jnp.stack([kap_below.astype(jnp.float32), kc[0]])
    k_xp = jnp.stack([kc[1], kap_above.astype(jnp.float32)])
    near = [k_zp, k_zm, jnp.roll(kc, -NZ, axis=-1), jnp.roll(kc, NZ, axis=-1), k_xm, k_xp]
    zmask = [zpos != NZ - 1, zpos != 0, True, True, True, True]
    w = [0.5 * (kc + k) for k in near]
    diag = w[0] + w[1] + w[2] + w[3] + w[4] + w[5]
    return jnp.stack([jnp.where(m, wt, 0.0) for m, wt in zip(zmask, w)] + [diag])


def chunked(values, nodes):
    chunk = values.shape[-1] // nodes
    zero = jnp.zeros(values.shape[:-1] + (NZ,), values.dtype)
    pieces = []
    for q in range(nodes):
        after = values[..., (q + 1) * chunk:(q + 1) * chunk + NZ] if q + 1 < nodes else zero
        before = values[..., q * chunk - NZ:q * chunk] if q > 0 else zero
        pieces.append(jnp.concatenate([values[..., q * chunk:(q + 1) * chunk], after, before], axis=-1))
    return jnp.stack(pieces, axis=-3)


def per_device(snapshots, kappa):
    rows, planes, width = snapshots.shape
    nodes = lax.axis_size("node")
    sizes = [lax.axis_size(a) for a in SPACE]
    spaces = math.prod(sizes)
    me = lax.axis_index("node")
    chunk = width // nodes
    span = chunk + 2 * NZ
    snaps = rows * nodes

    up = [(i, i + 1) for i in range(spaces - 1)]
    down = [(j, i) for i, j in up]

    kap_chunk = jnp.take(chunked(kappa[:, None], nodes)[:, :, 0], me, axis=1)
    kap_below = lax.ppermute(kap_chunk[1], SPACE, up)
    kap_above = lax.ppermute(kap_chunk[0], SPACE, down)
    coef = weights(kap_chunk, kap_below, kap_above)

    major = jnp.transpose(snapshots, (1, 0, 2))
    step = rows // GROUPS
    images, fields = [], []
    for g in range(GROUPS):
        pieces = chunked(major[:, g * step:(g + 1) * step], nodes)
        field = lax.all_to_all(pieces, "node", 1, 1, tiled=True).reshape(planes, nodes * step, span)
        below = lax.ppermute(field[1], SPACE, up)
        above = lax.ppermute(field[0], SPACE, down)
        images.append(stencil(field, below, above, coef))
        fields.append(field)
    dims = (((0, 2), (0, 2)), ((), ()))
    part = jnp.concatenate([
        jnp.concatenate([
            lax.dot_general(im, fd, dims, preferred_element_type=jnp.float32)
            for fd in fields], axis=1)
        for im in images], axis=0)
    part = part.reshape(GROUPS, nodes, step, snaps)
    total = jnp.take(part, me, axis=1)
    for d in range(1, nodes):
        blk = jnp.take(part, (me + d) % nodes, axis=1)
        total = total + lax.ppermute(blk, "node", [(i, (i + d) % nodes) for i in range(nodes)])
    total = total.reshape(rows, GROUPS, nodes, step).transpose(0, 2, 1, 3)
    total = total.reshape((rows,) + tuple(sizes) + (snaps // spaces,))
    for axis in reversed(range(len(SPACE))):
        total = jnp.moveaxis(total, axis + 1, 0)
        total = lax.all_to_all(total, SPACE[axis], 0, 0, tiled=True).sum(axis=0)
    out = total

    scale = jnp.float32(1.0 / math.sqrt(planes * spaces * NY * NZ))
    return out * scale


def solution(mesh):
    node, space = mesh.devices.shape
    cores = 2
    fine = Mesh(mesh.devices.reshape(node, space // (4 * cores), 4, cores), ("node",) + SPACE)
    placed = (P("node", SPACE, None), P(SPACE, None))
    return jax.shard_map(
        per_device, mesh=fine, in_specs=placed, out_specs=P("node", SPACE), check_vma=False
    )
```

```python
import math

import jax
import jax.numpy as jnp
from jax import lax
from jax.experimental import pallas as pl
from jax.experimental.pallas import tpu as pltpu
from jax.sharding import Mesh, PartitionSpec as P

NY = 128
NZ = 64
ROWS = 32
GROUPS = 2
SPACE = ("z", "y", "core")


def ahead(values, offset):
    tail = jnp.zeros(values.shape[:-1] + (offset,), values.dtype)
    return jnp.concatenate([values[..., offset:], tail], axis=-1)


def behind(values, offset):
    head = jnp.zeros(values.shape[:-1] + (offset,), values.dtype)
    return jnp.concatenate([head, values[..., :-offset]], axis=-1)


def stencil_kernel(x_ref, below_ref, above_ref, coef_ref, out_ref):
    span = below_ref.shape[1]
    lane = lax.broadcasted_iota(jnp.int32, (1, span), 1)
    inner = lane < span - 2 * NZ
    planes = [x_ref[p].astype(jnp.float32) for p in range(2)]
    below = below_ref[...].astype(jnp.float32)
    above = above_ref[...].astype(jnp.float32)
    for p in range(2):
        v = planes[p]

        def coef(t):
            return coef_ref[t, p:p + 1, :]

        near = coef(0) * pltpu.roll(v, span - 1, 1)
        near = near + coef(1) * pltpu.roll(v, 1, 1)
        near = near + coef(2) * pltpu.roll(v, span - NZ, 1)
        near = near + coef(3) * pltpu.roll(v, NZ, 1)
        near = near + coef(4) * (below if p == 0 else planes[0])
        near = near + coef(5) * (planes[1] if p == 0 else above)
        total = coef(6) * v - near
        out_ref[p] = jnp.where(inner, total, 0.0).astype(out_ref.dtype)


def stencil(field, below, above, coef):
    nodes, planes, step, span = field.shape
    return pl.pallas_call(
        stencil_kernel,
        grid=(nodes, step // ROWS),
        in_specs=[
            pl.BlockSpec((None, planes, ROWS, span), lambda a, i: (a, 0, i, 0)),
            pl.BlockSpec((None, ROWS, span), lambda a, i: (a, i, 0)),
            pl.BlockSpec((None, ROWS, span), lambda a, i: (a, i, 0)),
            pl.BlockSpec(coef.shape, lambda a, i: (0, 0, 0)),
        ],
        out_specs=pl.BlockSpec((None, planes, ROWS, span), lambda a, i: (a, 0, i, 0)),
        out_shape=jax.ShapeDtypeStruct(field.shape, jnp.bfloat16),
    )(field, below, above, coef)


def weights(kap_chunk, kap_below, kap_above):
    span = kap_chunk.shape[-1]
    kc = kap_chunk.astype(jnp.float32)
    zpos = jnp.arange(span, dtype=jnp.int32) % NZ
    k_zp = jnp.where(zpos != NZ - 1, jnp.roll(kc, -1, axis=-1), 0.0)
    k_zm = jnp.where(zpos != 0, jnp.roll(kc, 1, axis=-1), 0.0)
    k_xm = jnp.stack([kap_below.astype(jnp.float32), kc[0]])
    k_xp = jnp.stack([kc[1], kap_above.astype(jnp.float32)])
    near = [k_zp, k_zm, jnp.roll(kc, -NZ, axis=-1), jnp.roll(kc, NZ, axis=-1), k_xm, k_xp]
    zmask = [zpos != NZ - 1, zpos != 0, True, True, True, True]
    w = [0.5 * (kc + k) for k in near]
    diag = w[0] + w[1] + w[2] + w[3] + w[4] + w[5]
    return jnp.stack([jnp.where(m, wt, 0.0) for m, wt in zip(zmask, w)] + [diag])


def chunked(values, nodes):
    chunk = values.shape[-1] // nodes
    zero = jnp.zeros(values.shape[:-1] + (NZ,), values.dtype)
    pieces = []
    for q in range(nodes):
        after = values[..., (q + 1) * chunk:(q + 1) * chunk + NZ] if q + 1 < nodes else zero
        before = values[..., q * chunk - NZ:q * chunk] if q > 0 else zero
        pieces.append(jnp.concatenate([values[..., q * chunk:(q + 1) * chunk], after, before], axis=-1))
    return jnp.stack(pieces, axis=0)


def per_device(snapshots, kappa):
    rows, planes, width = snapshots.shape
    nodes = lax.axis_size("node")
    sizes = [lax.axis_size(a) for a in SPACE]
    spaces = math.prod(sizes)
    me = lax.axis_index("node")
    chunk = width // nodes
    span = chunk + 2 * NZ
    snaps = rows * nodes

    up = [(i, i + 1) for i in range(spaces - 1)]
    down = [(j, i) for i, j in up]

    kap_chunk = jnp.take(chunked(kappa[:, None], nodes), me, axis=0)[:, 0]
    kap_below = lax.ppermute(kap_chunk[1], SPACE, up)
    kap_above = lax.ppermute(kap_chunk[0], SPACE, down)
    coef = weights(kap_chunk, kap_below, kap_above)

    major = jnp.transpose(snapshots, (1, 0, 2))
    step = rows // GROUPS
    images, fields = [], []
    for g in range(GROUPS):
        pieces = chunked(major[:, g * step:(g + 1) * step], nodes)
        field = lax.all_to_all(pieces, "node", 0, 0, tiled=True)
        below = lax.ppermute(field[:, 1], SPACE, up)
        above = lax.ppermute(field[:, 0], SPACE, down)
        images.append(stencil(field, below, above, coef))
        fields.append(field)
    dims = (((1, 3), (1, 3)), ((), ()))
    part = jnp.concatenate([
        jnp.concatenate([
            lax.dot_general(im, fd, dims, preferred_element_type=jnp.float32).reshape(nodes * step, nodes * step)
            for fd in fields], axis=1)
        for im in images], axis=0)
    part = part.reshape(snaps, snaps)
    part = part.reshape(GROUPS, nodes, step, snaps)
    total = jnp.take(part, me, axis=1)
    for d in range(1, nodes):
        blk = jnp.take(part, (me + d) % nodes, axis=1)
        total = total + lax.ppermute(blk, "node", [(i, (i + d) % nodes) for i in range(nodes)])
    total = total.reshape(rows, GROUPS, nodes, step).transpose(0, 2, 1, 3)
    total = total.reshape((rows,) + tuple(sizes) + (snaps // spaces,))
    for axis in reversed(range(len(SPACE))):
        total = jnp.moveaxis(total, axis + 1, 0)
        total = lax.all_to_all(total, SPACE[axis], 0, 0, tiled=True).sum(axis=0)
    out = total

    scale = jnp.float32(1.0 / math.sqrt(planes * spaces * NY * NZ))
    return out * scale


def solution(mesh):
    node, space = mesh.devices.shape
    cores = 2
    fine = Mesh(mesh.devices.reshape(node, space // (4 * cores), 4, cores), ("node",) + SPACE)
    placed = (P("node", SPACE, None), P(SPACE, None))
    return jax.shard_map(
        per_device, mesh=fine, in_specs=placed, out_specs=P("node", SPACE), check_vma=False
    )
```

```python
import math

import jax
import jax.numpy as jnp
from jax import lax
from jax.experimental import pallas as pl
from jax.experimental.pallas import tpu as pltpu
from jax.sharding import Mesh, PartitionSpec as P

NY = 128
NZ = 64
ROWS = 32
GROUPS = 4
SPACE = ("z", "y", "core")


def ahead(values, offset):
    tail = jnp.zeros(values.shape[:-1] + (offset,), values.dtype)
    return jnp.concatenate([values[..., offset:], tail], axis=-1)


def behind(values, offset):
    head = jnp.zeros(values.shape[:-1] + (offset,), values.dtype)
    return jnp.concatenate([head, values[..., :-offset]], axis=-1)


def stencil_kernel(x_ref, below_ref, above_ref, coef_ref, out_ref):
    span = below_ref.shape[1]
    lane = lax.broadcasted_iota(jnp.int32, (1, span), 1)
    inner = lane < span - 2 * NZ
    planes = [x_ref[p].astype(jnp.float32) for p in range(2)]
    below = below_ref[...].astype(jnp.float32)
    above = above_ref[...].astype(jnp.float32)
    for p in range(2):
        v = planes[p]

        def coef(t):
            return coef_ref[t, p:p + 1, :]

        near = coef(0) * pltpu.roll(v, span - 1, 1)
        near = near + coef(1) * pltpu.roll(v, 1, 1)
        near = near + coef(2) * pltpu.roll(v, span - NZ, 1)
        near = near + coef(3) * pltpu.roll(v, NZ, 1)
        near = near + coef(4) * (below if p == 0 else planes[0])
        near = near + coef(5) * (planes[1] if p == 0 else above)
        total = coef(6) * v - near
        out_ref[p] = jnp.where(inner, total, 0.0).astype(out_ref.dtype)


def stencil(field, below, above, coef):
    planes, snaps, span = field.shape
    return pl.pallas_call(
        stencil_kernel,
        grid=(snaps // ROWS,),
        in_specs=[
            pl.BlockSpec((planes, ROWS, span), lambda i: (0, i, 0)),
            pl.BlockSpec((ROWS, span), lambda i: (i, 0)),
            pl.BlockSpec((ROWS, span), lambda i: (i, 0)),
            pl.BlockSpec(coef.shape, lambda i: (0, 0, 0)),
        ],
        out_specs=pl.BlockSpec((planes, ROWS, span), lambda i: (0, i, 0)),
        out_shape=jax.ShapeDtypeStruct(field.shape, jnp.bfloat16),
    )(field, below, above, coef)


def weights(kap_chunk, kap_below, kap_above):
    span = kap_chunk.shape[-1]
    kc = kap_chunk.astype(jnp.float32)
    zpos = jnp.arange(span, dtype=jnp.int32) % NZ
    k_zp = jnp.where(zpos != NZ - 1, jnp.roll(kc, -1, axis=-1), 0.0)
    k_zm = jnp.where(zpos != 0, jnp.roll(kc, 1, axis=-1), 0.0)
    k_xm = jnp.stack([kap_below.astype(jnp.float32), kc[0]])
    k_xp = jnp.stack([kc[1], kap_above.astype(jnp.float32)])
    near = [k_zp, k_zm, jnp.roll(kc, -NZ, axis=-1), jnp.roll(kc, NZ, axis=-1), k_xm, k_xp]
    zmask = [zpos != NZ - 1, zpos != 0, True, True, True, True]
    w = [0.5 * (kc + k) for k in near]
    diag = w[0] + w[1] + w[2] + w[3] + w[4] + w[5]
    return jnp.stack([jnp.where(m, wt, 0.0) for m, wt in zip(zmask, w)] + [diag])


def chunked(values, nodes):
    chunk = values.shape[-1] // nodes
    zero = jnp.zeros(values.shape[:-1] + (NZ,), values.dtype)
    pieces = []
    for q in range(nodes):
        after = values[..., (q + 1) * chunk:(q + 1) * chunk + NZ] if q + 1 < nodes else zero
        before = values[..., q * chunk - NZ:q * chunk] if q > 0 else zero
        pieces.append(jnp.concatenate([values[..., q * chunk:(q + 1) * chunk], after, before], axis=-1))
    return jnp.stack(pieces, axis=-3)


def per_device(snapshots, kappa):
    rows, planes, width = snapshots.shape
    nodes = lax.axis_size("node")
    sizes = [lax.axis_size(a) for a in SPACE]
    spaces = math.prod(sizes)
    me = lax.axis_index("node")
    chunk = width // nodes
    span = chunk + 2 * NZ
    snaps = rows * nodes

    up = [(i, i + 1) for i in range(spaces - 1)]
    down = [(j, i) for i, j in up]

    kap_chunk = jnp.take(chunked(kappa[:, None], nodes)[:, :, 0], me, axis=1)
    kap_below = lax.ppermute(kap_chunk[1], SPACE, up)
    kap_above = lax.ppermute(kap_chunk[0], SPACE, down)
    coef = weights(kap_chunk, kap_below, kap_above)

    major = jnp.transpose(snapshots, (1, 0, 2))
    step = rows // GROUPS
    images, fields = [], []
    for g in range(GROUPS):
        pieces = chunked(major[:, g * step:(g + 1) * step], nodes)
        field = lax.all_to_all(pieces, "node", 1, 1, tiled=True).reshape(planes, nodes * step, span)
        below = lax.ppermute(field[1], SPACE, up)
        above = lax.ppermute(field[0], SPACE, down)
        images.append(stencil(field, below, above, coef))
        fields.append(field)
    dims = (((0, 2), (0, 2)), ((), ()))
    part = jnp.concatenate([
        jnp.concatenate([
            lax.dot_general(im, fd, dims, preferred_element_type=jnp.float32)
            for fd in fields], axis=1)
        for im in images], axis=0)
    part = part.reshape(GROUPS, nodes, step, snaps)
    total = jnp.take(part, me, axis=1)
    for d in range(1, nodes):
        blk = jnp.take(part, (me + d) % nodes, axis=1)
        total = total + lax.ppermute(blk, "node", [(i, (i + d) % nodes) for i in range(nodes)])
    total = total.reshape(rows, GROUPS, nodes, step).transpose(0, 2, 1, 3)
    total = total.reshape((rows,) + tuple(sizes) + (snaps // spaces,))
    for axis in reversed(range(len(SPACE))):
        total = jnp.moveaxis(total, axis + 1, 0)
        total = lax.all_to_all(total, SPACE[axis], 0, 0, tiled=True).sum(axis=0)
    out = total

    scale = jnp.float32(1.0 / math.sqrt(planes * spaces * NY * NZ))
    return out * scale


def solution(mesh):
    node, space = mesh.devices.shape
    cores = 2
    fine = Mesh(mesh.devices.reshape(node, space // (4 * cores), 4, cores), ("node",) + SPACE)
    placed = (P("node", SPACE, None), P(SPACE, None))
    return jax.shard_map(
        per_device, mesh=fine, in_specs=placed, out_specs=P("node", SPACE), check_vma=False
    )
```

```python
import math

import jax
import jax.numpy as jnp
from jax import lax
from jax.experimental import pallas as pl
from jax.experimental.pallas import tpu as pltpu
from jax.sharding import Mesh, PartitionSpec as P

NY = 128
NZ = 64
ROWS = 32
GROUPS = 2
SPACE = ("z", "y", "core")


def ahead(values, offset):
    tail = jnp.zeros(values.shape[:-1] + (offset,), values.dtype)
    return jnp.concatenate([values[..., offset:], tail], axis=-1)


def behind(values, offset):
    head = jnp.zeros(values.shape[:-1] + (offset,), values.dtype)
    return jnp.concatenate([head, values[..., :-offset]], axis=-1)


def stencil_kernel(x_ref, below_ref, above_ref, coef_ref, out_ref):
    span = below_ref.shape[1]
    lane = lax.broadcasted_iota(jnp.int32, (1, span), 1)
    inner = lane < span - 2 * NZ
    planes = [x_ref[p].astype(jnp.float32) for p in range(2)]
    below = below_ref[...].astype(jnp.float32)
    above = above_ref[...].astype(jnp.float32)
    for p in range(2):
        v = planes[p]

        def coef(t):
            return coef_ref[t, p:p + 1, :]

        near = coef(0) * pltpu.roll(v, span - 1, 1)
        near = near + coef(1) * pltpu.roll(v, 1, 1)
        near = near + coef(2) * pltpu.roll(v, span - NZ, 1)
        near = near + coef(3) * pltpu.roll(v, NZ, 1)
        near = near + coef(4) * (below if p == 0 else planes[0])
        near = near + coef(5) * (planes[1] if p == 0 else above)
        total = coef(6) * v - near
        out_ref[p] = jnp.where(inner, total, 0.0).astype(out_ref.dtype)


def stencil(field, below, above, coef):
    planes, snaps, span = field.shape
    return pl.pallas_call(
        stencil_kernel,
        grid=(snaps // ROWS,),
        in_specs=[
            pl.BlockSpec((planes, ROWS, span), lambda i: (0, i, 0)),
            pl.BlockSpec((ROWS, span), lambda i: (i, 0)),
            pl.BlockSpec((ROWS, span), lambda i: (i, 0)),
            pl.BlockSpec(coef.shape, lambda i: (0, 0, 0)),
        ],
        out_specs=pl.BlockSpec((planes, ROWS, span), lambda i: (0, i, 0)),
        out_shape=jax.ShapeDtypeStruct(field.shape, jnp.bfloat16),
    )(field, below, above, coef)


def weights(kap_chunk, kap_below, kap_above):
    span = kap_chunk.shape[-1]
    kc = kap_chunk.astype(jnp.float32)
    zpos = jnp.arange(span, dtype=jnp.int32) % NZ
    k_zp = jnp.where(zpos != NZ - 1, jnp.roll(kc, -1, axis=-1), 0.0)
    k_zm = jnp.where(zpos != 0, jnp.roll(kc, 1, axis=-1), 0.0)
    k_xm = jnp.stack([kap_below.astype(jnp.float32), kc[0]])
    k_xp = jnp.stack([kc[1], kap_above.astype(jnp.float32)])
    near = [k_zp, k_zm, jnp.roll(kc, -NZ, axis=-1), jnp.roll(kc, NZ, axis=-1), k_xm, k_xp]
    zmask = [zpos != NZ - 1, zpos != 0, True, True, True, True]
    w = [0.5 * (kc + k) for k in near]
    diag = w[0] + w[1] + w[2] + w[3] + w[4] + w[5]
    return jnp.stack([jnp.where(m, wt, 0.0) for m, wt in zip(zmask, w)] + [diag])


def chunked(values, nodes):
    chunk = values.shape[-1] // nodes
    zero = jnp.zeros(values.shape[:-1] + (NZ,), values.dtype)
    pieces = []
    for q in range(nodes):
        after = values[..., (q + 1) * chunk:(q + 1) * chunk + NZ] if q + 1 < nodes else zero
        before = values[..., q * chunk - NZ:q * chunk] if q > 0 else zero
        pieces.append(jnp.concatenate([values[..., q * chunk:(q + 1) * chunk], after, before], axis=-1))
    return jnp.stack(pieces, axis=-3)


def per_device(snapshots, kappa):
    rows, planes, width = snapshots.shape
    nodes = lax.axis_size("node")
    sizes = [lax.axis_size(a) for a in SPACE]
    spaces = math.prod(sizes)
    me = lax.axis_index("node")
    chunk = width // nodes
    span = chunk + 2 * NZ
    snaps = rows * nodes

    up = [(i, i + 1) for i in range(spaces - 1)]
    down = [(j, i) for i, j in up]

    step = rows // GROUPS
    images, fields, fronts = [], [], []
    for g in range(GROUPS):
        major = jnp.transpose(snapshots[g * step:(g + 1) * step], (1, 0, 2))
        field = lax.all_to_all(chunked(major, nodes), "node", 1, 1, tiled=True).reshape(planes, nodes * step, span)
        below = lax.ppermute(field[1], SPACE, up)
        above = lax.ppermute(field[0], SPACE, down)
        fields.append(field)
        fronts.append((below, above))
        if g == 0:
            late, _ = lax.optimization_barrier((kappa, field))
            kap_chunk = jnp.take(chunked(late[:, None], nodes)[:, :, 0], me, axis=1)
            kap_below = lax.ppermute(kap_chunk[1], SPACE, up)
            kap_above = lax.ppermute(kap_chunk[0], SPACE, down)
            coef = weights(kap_chunk, kap_below, kap_above)
    for field, (below, above) in zip(fields, fronts):
        images.append(stencil(field, below, above, coef))
    dims = (((0, 2), (0, 2)), ((), ()))
    part = jnp.concatenate([
        jnp.concatenate([
            lax.dot_general(im, fd, dims, preferred_element_type=jnp.float32)
            for fd in fields], axis=1)
        for im in images], axis=0)
    part = part.reshape(GROUPS, nodes, step, snaps)
    total = jnp.take(part, me, axis=1)
    for d in range(1, nodes):
        blk = jnp.take(part, (me + d) % nodes, axis=1)
        total = total + lax.ppermute(blk, "node", [(i, (i + d) % nodes) for i in range(nodes)])
    total = total.reshape(rows, GROUPS, nodes, step).transpose(0, 2, 1, 3)
    total = total.reshape((rows,) + tuple(sizes) + (snaps // spaces,))
    for axis in reversed(range(len(SPACE))):
        total = jnp.moveaxis(total, axis + 1, 0)
        total = lax.all_to_all(total, SPACE[axis], 0, 0, tiled=True).sum(axis=0)
    out = total

    scale = jnp.float32(1.0 / math.sqrt(planes * spaces * NY * NZ))
    return out * scale


def solution(mesh):
    node, space = mesh.devices.shape
    cores = 2
    fine = Mesh(mesh.devices.reshape(node, space // (4 * cores), 4, cores), ("node",) + SPACE)
    placed = (P("node", SPACE, None), P(SPACE, None))
    return jax.shard_map(
        per_device, mesh=fine, in_specs=placed, out_specs=P("node", SPACE), check_vma=False
    )
```

```python
import math

import jax
import jax.numpy as jnp
from jax import lax
from jax.experimental import pallas as pl
from jax.experimental.pallas import tpu as pltpu
from jax.sharding import Mesh, PartitionSpec as P

NY = 128
NZ = 64
ROWS = 32
GROUPS = 2
SPACE = ("z", "y", "core")


def ahead(values, offset):
    tail = jnp.zeros(values.shape[:-1] + (offset,), values.dtype)
    return jnp.concatenate([values[..., offset:], tail], axis=-1)


def behind(values, offset):
    head = jnp.zeros(values.shape[:-1] + (offset,), values.dtype)
    return jnp.concatenate([head, values[..., :-offset]], axis=-1)


def stencil_kernel(x_ref, below_ref, above_ref, coef_ref, out_ref, copy_ref):
    span = below_ref.shape[1]
    lane = lax.broadcasted_iota(jnp.int32, (1, span), 1)
    inner = lane < span - 2 * NZ
    copy_ref[...] = x_ref[...]
    planes = [x_ref[p].astype(jnp.float32) for p in range(2)]
    below = below_ref[...].astype(jnp.float32)
    above = above_ref[...].astype(jnp.float32)
    for p in range(2):
        v = planes[p]

        def coef(t):
            return coef_ref[t, p:p + 1, :]

        near = coef(0) * pltpu.roll(v, span - 1, 1)
        near = near + coef(1) * pltpu.roll(v, 1, 1)
        near = near + coef(2) * pltpu.roll(v, span - NZ, 1)
        near = near + coef(3) * pltpu.roll(v, NZ, 1)
        near = near + coef(4) * (below if p == 0 else planes[0])
        near = near + coef(5) * (planes[1] if p == 0 else above)
        total = coef(6) * v - near
        out_ref[p] = jnp.where(inner, total, 0.0).astype(out_ref.dtype)


def stencil(field, below, above, coef):
    nodes, planes, step, span = field.shape
    blocks = step // ROWS
    out_spec = pl.BlockSpec((planes, ROWS, span), lambda a, i: (0, a * blocks + i, 0))
    flat = jax.ShapeDtypeStruct((planes, nodes * step, span), jnp.bfloat16)
    return pl.pallas_call(
        stencil_kernel,
        grid=(nodes, blocks),
        in_specs=[
            pl.BlockSpec((None, planes, ROWS, span), lambda a, i: (a, 0, i, 0)),
            pl.BlockSpec((None, ROWS, span), lambda a, i: (a, i, 0)),
            pl.BlockSpec((None, ROWS, span), lambda a, i: (a, i, 0)),
            pl.BlockSpec(coef.shape, lambda a, i: (0, 0, 0)),
        ],
        out_specs=[out_spec, out_spec],
        out_shape=[flat, flat],
    )(field, below, above, coef)


def weights(kap_chunk, kap_below, kap_above):
    span = kap_chunk.shape[-1]
    kc = kap_chunk.astype(jnp.float32)
    zpos = jnp.arange(span, dtype=jnp.int32) % NZ
    k_zp = jnp.where(zpos != NZ - 1, jnp.roll(kc, -1, axis=-1), 0.0)
    k_zm = jnp.where(zpos != 0, jnp.roll(kc, 1, axis=-1), 0.0)
    k_xm = jnp.stack([kap_below.astype(jnp.float32), kc[0]])
    k_xp = jnp.stack([kc[1], kap_above.astype(jnp.float32)])
    near = [k_zp, k_zm, jnp.roll(kc, -NZ, axis=-1), jnp.roll(kc, NZ, axis=-1), k_xm, k_xp]
    zmask = [zpos != NZ - 1, zpos != 0, True, True, True, True]
    w = [0.5 * (kc + k) for k in near]
    diag = w[0] + w[1] + w[2] + w[3] + w[4] + w[5]
    return jnp.stack([jnp.where(m, wt, 0.0) for m, wt in zip(zmask, w)] + [diag])


def chunked(values, nodes):
    chunk = values.shape[-1] // nodes
    zero = jnp.zeros(values.shape[:-1] + (NZ,), values.dtype)
    pieces = []
    for q in range(nodes):
        after = values[..., (q + 1) * chunk:(q + 1) * chunk + NZ] if q + 1 < nodes else zero
        before = values[..., q * chunk - NZ:q * chunk] if q > 0 else zero
        pieces.append(jnp.concatenate([values[..., q * chunk:(q + 1) * chunk], after, before], axis=-1))
    return jnp.stack(pieces, axis=0)


def per_device(snapshots, kappa):
    rows, planes, width = snapshots.shape
    nodes = lax.axis_size("node")
    sizes = [lax.axis_size(a) for a in SPACE]
    spaces = math.prod(sizes)
    me = lax.axis_index("node")
    chunk = width // nodes
    span = chunk + 2 * NZ
    snaps = rows * nodes

    up = [(i, i + 1) for i in range(spaces - 1)]
    down = [(j, i) for i, j in up]

    step = rows // GROUPS
    images, fields, fronts = [], [], []
    for g in range(GROUPS):
        major = jnp.transpose(snapshots[g * step:(g + 1) * step], (1, 0, 2))
        field = lax.all_to_all(chunked(major, nodes), "node", 0, 0, tiled=True)
        below = lax.ppermute(field[:, 1], SPACE, up)
        above = lax.ppermute(field[:, 0], SPACE, down)
        fields.append(field)
        fronts.append((below, above))
        if g == 0:
            late, _ = lax.optimization_barrier((kappa, field))
            kap_chunk = jnp.take(chunked(late[:, None], nodes), me, axis=0)[:, 0]
            kap_below = lax.ppermute(kap_chunk[1], SPACE, up)
            kap_above = lax.ppermute(kap_chunk[0], SPACE, down)
            coef = weights(kap_chunk, kap_below, kap_above)
    for g, (below, above) in enumerate(fronts):
        image, fields[g] = stencil(fields[g], below, above, coef)
        images.append(image)
    dims = (((0, 2), (0, 2)), ((), ()))
    part = jnp.concatenate([
        jnp.concatenate([
            lax.dot_general(im, fd, dims, preferred_element_type=jnp.float32)
            for fd in fields], axis=1)
        for im in images], axis=0)
    part = part.reshape(GROUPS, nodes, step, snaps)
    total = jnp.take(part, me, axis=1)
    for d in range(1, nodes):
        blk = jnp.take(part, (me + d) % nodes, axis=1)
        total = total + lax.ppermute(blk, "node", [(i, (i + d) % nodes) for i in range(nodes)])
    total = total.reshape(rows, GROUPS, nodes, step).transpose(0, 2, 1, 3)
    total = total.reshape((rows,) + tuple(sizes) + (snaps // spaces,))
    for axis in reversed(range(len(SPACE))):
        total = jnp.moveaxis(total, axis + 1, 0)
        total = lax.all_to_all(total, SPACE[axis], 0, 0, tiled=True).sum(axis=0)
    out = total

    scale = jnp.float32(1.0 / math.sqrt(planes * spaces * NY * NZ))
    return out * scale


def solution(mesh):
    node, space = mesh.devices.shape
    cores = 2
    fine = Mesh(mesh.devices.reshape(node, space // (4 * cores), 4, cores), ("node",) + SPACE)
    placed = (P("node", SPACE, None), P(SPACE, None))
    return jax.shard_map(
        per_device, mesh=fine, in_specs=placed, out_specs=P("node", SPACE), check_vma=False
    )
```

```python
import math

import jax
import jax.numpy as jnp
from jax import lax
from jax.experimental import pallas as pl
from jax.experimental.pallas import tpu as pltpu
from jax.sharding import Mesh, PartitionSpec as P

NY = 128
NZ = 64
ROWS = 64
GROUPS = 2
SPACE = ("z", "y", "core")


def ahead(values, offset):
    tail = jnp.zeros(values.shape[:-1] + (offset,), values.dtype)
    return jnp.concatenate([values[..., offset:], tail], axis=-1)


def behind(values, offset):
    head = jnp.zeros(values.shape[:-1] + (offset,), values.dtype)
    return jnp.concatenate([head, values[..., :-offset]], axis=-1)


def stencil_kernel(x_ref, below_ref, above_ref, coef_ref, out_ref):
    span = below_ref.shape[1]
    lane = lax.broadcasted_iota(jnp.int32, (1, span), 1)
    inner = lane < span - 2 * NZ
    planes = [x_ref[p].astype(jnp.float32) for p in range(2)]
    below = below_ref[...].astype(jnp.float32)
    above = above_ref[...].astype(jnp.float32)
    for p in range(2):
        v = planes[p]

        def coef(t):
            return coef_ref[t, p:p + 1, :]

        near = coef(0) * pltpu.roll(v, span - 1, 1)
        near = near + coef(1) * pltpu.roll(v, 1, 1)
        near = near + coef(2) * pltpu.roll(v, span - NZ, 1)
        near = near + coef(3) * pltpu.roll(v, NZ, 1)
        near = near + coef(4) * (below if p == 0 else planes[0])
        near = near + coef(5) * (planes[1] if p == 0 else above)
        total = coef(6) * v - near
        out_ref[p] = jnp.where(inner, total, 0.0).astype(out_ref.dtype)


def stencil(field, below, above, coef):
    planes, snaps, span = field.shape
    return pl.pallas_call(
        stencil_kernel,
        grid=(snaps // ROWS,),
        in_specs=[
            pl.BlockSpec((planes, ROWS, span), lambda i: (0, i, 0)),
            pl.BlockSpec((ROWS, span), lambda i: (i, 0)),
            pl.BlockSpec((ROWS, span), lambda i: (i, 0)),
            pl.BlockSpec(coef.shape, lambda i: (0, 0, 0)),
        ],
        out_specs=pl.BlockSpec((planes, ROWS, span), lambda i: (0, i, 0)),
        out_shape=jax.ShapeDtypeStruct(field.shape, jnp.bfloat16),
    )(field, below, above, coef)


def weights(kap_chunk, kap_below, kap_above):
    span = kap_chunk.shape[-1]
    kc = kap_chunk.astype(jnp.float32)
    zpos = jnp.arange(span, dtype=jnp.int32) % NZ
    k_zp = jnp.where(zpos != NZ - 1, jnp.roll(kc, -1, axis=-1), 0.0)
    k_zm = jnp.where(zpos != 0, jnp.roll(kc, 1, axis=-1), 0.0)
    k_xm = jnp.stack([kap_below.astype(jnp.float32), kc[0]])
    k_xp = jnp.stack([kc[1], kap_above.astype(jnp.float32)])
    near = [k_zp, k_zm, jnp.roll(kc, -NZ, axis=-1), jnp.roll(kc, NZ, axis=-1), k_xm, k_xp]
    zmask = [zpos != NZ - 1, zpos != 0, True, True, True, True]
    w = [0.5 * (kc + k) for k in near]
    diag = w[0] + w[1] + w[2] + w[3] + w[4] + w[5]
    return jnp.stack([jnp.where(m, wt, 0.0) for m, wt in zip(zmask, w)] + [diag])


def chunked(values, nodes):
    chunk = values.shape[-1] // nodes
    zero = jnp.zeros(values.shape[:-1] + (NZ,), values.dtype)
    pieces = []
    for q in range(nodes):
        after = values[..., (q + 1) * chunk:(q + 1) * chunk + NZ] if q + 1 < nodes else zero
        before = values[..., q * chunk - NZ:q * chunk] if q > 0 else zero
        pieces.append(jnp.concatenate([values[..., q * chunk:(q + 1) * chunk], after, before], axis=-1))
    return jnp.stack(pieces, axis=-3)


def per_device(snapshots, kappa):
    rows, planes, width = snapshots.shape
    nodes = lax.axis_size("node")
    sizes = [lax.axis_size(a) for a in SPACE]
    spaces = math.prod(sizes)
    me = lax.axis_index("node")
    chunk = width // nodes
    span = chunk + 2 * NZ
    snaps = rows * nodes

    up = [(i, i + 1) for i in range(spaces - 1)]
    down = [(j, i) for i, j in up]

    step = rows // GROUPS
    images, fields, fronts = [], [], []
    for g in range(GROUPS):
        major = jnp.transpose(snapshots[g * step:(g + 1) * step], (1, 0, 2))
        field = lax.all_to_all(chunked(major, nodes), "node", 1, 1, tiled=True).reshape(planes, nodes * step, span)
        below = lax.ppermute(field[1], SPACE, up)
        above = lax.ppermute(field[0], SPACE, down)
        fields.append(field)
        fronts.append((below, above))
        if g == 0:
            late, _ = lax.optimization_barrier((kappa, field))
            kap_chunk = jnp.take(chunked(late[:, None], nodes)[:, :, 0], me, axis=1)
            kap_below = lax.ppermute(kap_chunk[1], SPACE, up)
            kap_above = lax.ppermute(kap_chunk[0], SPACE, down)
            coef = weights(kap_chunk, kap_below, kap_above)
    for field, (below, above) in zip(fields, fronts):
        images.append(stencil(field, below, above, coef))
    dims = (((0, 2), (0, 2)), ((), ()))
    part = jnp.concatenate([
        jnp.concatenate([
            lax.dot_general(im, fd, dims, preferred_element_type=jnp.float32)
            for fd in fields], axis=1)
        for im in images], axis=0)
    part = part.reshape(GROUPS, nodes, step, snaps)
    total = jnp.take(part, me, axis=1)
    for d in range(1, nodes):
        blk = jnp.take(part, (me + d) % nodes, axis=1)
        total = total + lax.ppermute(blk, "node", [(i, (i + d) % nodes) for i in range(nodes)])
    total = total.reshape(rows, GROUPS, nodes, step).transpose(0, 2, 1, 3)
    total = total.reshape((rows,) + tuple(sizes) + (snaps // spaces,))
    for axis in reversed(range(len(SPACE))):
        total = jnp.moveaxis(total, axis + 1, 0)
        total = lax.all_to_all(total, SPACE[axis], 0, 0, tiled=True).sum(axis=0)
    out = total

    scale = jnp.float32(1.0 / math.sqrt(planes * spaces * NY * NZ))
    return out * scale


def solution(mesh):
    node, space = mesh.devices.shape
    cores = 2
    fine = Mesh(mesh.devices.reshape(node, space // (4 * cores), 4, cores), ("node",) + SPACE)
    placed = (P("node", SPACE, None), P(SPACE, None))
    return jax.shard_map(
        per_device, mesh=fine, in_specs=placed, out_specs=P("node", SPACE), check_vma=False
    )
```

```python
import math

import jax
import jax.numpy as jnp
from jax import lax
from jax.experimental import pallas as pl
from jax.experimental.pallas import tpu as pltpu
from jax.sharding import Mesh, PartitionSpec as P

NY = 128
NZ = 64
ROWS = 128
GROUPS = 2
SPACE = ("z", "y", "core")


def ahead(values, offset):
    tail = jnp.zeros(values.shape[:-1] + (offset,), values.dtype)
    return jnp.concatenate([values[..., offset:], tail], axis=-1)


def behind(values, offset):
    head = jnp.zeros(values.shape[:-1] + (offset,), values.dtype)
    return jnp.concatenate([head, values[..., :-offset]], axis=-1)


def stencil_kernel(x_ref, below_ref, above_ref, coef_ref, out_ref):
    span = below_ref.shape[1]
    lane = lax.broadcasted_iota(jnp.int32, (1, span), 1)
    inner = lane < span - 2 * NZ
    planes = [x_ref[p].astype(jnp.float32) for p in range(2)]
    below = below_ref[...].astype(jnp.float32)
    above = above_ref[...].astype(jnp.float32)
    for p in range(2):
        v = planes[p]

        def coef(t):
            return coef_ref[t, p:p + 1, :]

        near = coef(0) * pltpu.roll(v, span - 1, 1)
        near = near + coef(1) * pltpu.roll(v, 1, 1)
        near = near + coef(2) * pltpu.roll(v, span - NZ, 1)
        near = near + coef(3) * pltpu.roll(v, NZ, 1)
        near = near + coef(4) * (below if p == 0 else planes[0])
        near = near + coef(5) * (planes[1] if p == 0 else above)
        total = coef(6) * v - near
        out_ref[p] = jnp.where(inner, total, 0.0).astype(out_ref.dtype)


def stencil(field, below, above, coef):
    planes, snaps, span = field.shape
    return pl.pallas_call(
        stencil_kernel,
        grid=(snaps // ROWS,),
        in_specs=[
            pl.BlockSpec((planes, ROWS, span), lambda i: (0, i, 0)),
            pl.BlockSpec((ROWS, span), lambda i: (i, 0)),
            pl.BlockSpec((ROWS, span), lambda i: (i, 0)),
            pl.BlockSpec(coef.shape, lambda i: (0, 0, 0)),
        ],
        out_specs=pl.BlockSpec((planes, ROWS, span), lambda i: (0, i, 0)),
        out_shape=jax.ShapeDtypeStruct(field.shape, jnp.bfloat16),
    )(field, below, above, coef)


def weights(kap_chunk, kap_below, kap_above):
    span = kap_chunk.shape[-1]
    kc = kap_chunk.astype(jnp.float32)
    zpos = jnp.arange(span, dtype=jnp.int32) % NZ
    k_zp = jnp.where(zpos != NZ - 1, jnp.roll(kc, -1, axis=-1), 0.0)
    k_zm = jnp.where(zpos != 0, jnp.roll(kc, 1, axis=-1), 0.0)
    k_xm = jnp.stack([kap_below.astype(jnp.float32), kc[0]])
    k_xp = jnp.stack([kc[1], kap_above.astype(jnp.float32)])
    near = [k_zp, k_zm, jnp.roll(kc, -NZ, axis=-1), jnp.roll(kc, NZ, axis=-1), k_xm, k_xp]
    zmask = [zpos != NZ - 1, zpos != 0, True, True, True, True]
    w = [0.5 * (kc + k) for k in near]
    diag = w[0] + w[1] + w[2] + w[3] + w[4] + w[5]
    return jnp.stack([jnp.where(m, wt, 0.0) for m, wt in zip(zmask, w)] + [diag])


def chunked(values, nodes):
    chunk = values.shape[-1] // nodes
    zero = jnp.zeros(values.shape[:-1] + (NZ,), values.dtype)
    pieces = []
    for q in range(nodes):
        after = values[..., (q + 1) * chunk:(q + 1) * chunk + NZ] if q + 1 < nodes else zero
        before = values[..., q * chunk - NZ:q * chunk] if q > 0 else zero
        pieces.append(jnp.concatenate([values[..., q * chunk:(q + 1) * chunk], after, before], axis=-1))
    return jnp.stack(pieces, axis=-3)


def per_device(snapshots, kappa):
    rows, planes, width = snapshots.shape
    nodes = lax.axis_size("node")
    sizes = [lax.axis_size(a) for a in SPACE]
    spaces = math.prod(sizes)
    me = lax.axis_index("node")
    chunk = width // nodes
    span = chunk + 2 * NZ
    snaps = rows * nodes

    up = [(i, i + 1) for i in range(spaces - 1)]
    down = [(j, i) for i, j in up]

    step = rows // GROUPS
    images, fields, fronts = [], [], []
    for g in range(GROUPS):
        major = jnp.transpose(snapshots[g * step:(g + 1) * step], (1, 0, 2))
        field = lax.all_to_all(chunked(major, nodes), "node", 1, 1, tiled=True).reshape(planes, nodes * step, span)
        below = lax.ppermute(field[1], SPACE, up)
        above = lax.ppermute(field[0], SPACE, down)
        fields.append(field)
        fronts.append((below, above))
        if g == 0:
            late, _ = lax.optimization_barrier((kappa, field))
            kap_chunk = jnp.take(chunked(late[:, None], nodes)[:, :, 0], me, axis=1)
            kap_below = lax.ppermute(kap_chunk[1], SPACE, up)
            kap_above = lax.ppermute(kap_chunk[0], SPACE, down)
            coef = weights(kap_chunk, kap_below, kap_above)
    for field, (below, above) in zip(fields, fronts):
        images.append(stencil(field, below, above, coef))
    dims = (((0, 2), (0, 2)), ((), ()))
    part = jnp.concatenate([
        jnp.concatenate([
            lax.dot_general(im, fd, dims, preferred_element_type=jnp.float32)
            for fd in fields], axis=1)
        for im in images], axis=0)
    part = part.reshape(GROUPS, nodes, step, snaps)
    total = jnp.take(part, me, axis=1)
    for d in range(1, nodes):
        blk = jnp.take(part, (me + d) % nodes, axis=1)
        total = total + lax.ppermute(blk, "node", [(i, (i + d) % nodes) for i in range(nodes)])
    total = total.reshape(rows, GROUPS, nodes, step).transpose(0, 2, 1, 3)
    total = total.reshape((rows,) + tuple(sizes) + (snaps // spaces,))
    for axis in reversed(range(len(SPACE))):
        total = jnp.moveaxis(total, axis + 1, 0)
        total = lax.all_to_all(total, SPACE[axis], 0, 0, tiled=True).sum(axis=0)
    out = total

    scale = jnp.float32(1.0 / math.sqrt(planes * spaces * NY * NZ))
    return out * scale


def solution(mesh):
    node, space = mesh.devices.shape
    cores = 2
    fine = Mesh(mesh.devices.reshape(node, space // (4 * cores), 4, cores), ("node",) + SPACE)
    placed = (P("node", SPACE, None), P(SPACE, None))
    return jax.shard_map(
        per_device, mesh=fine, in_specs=placed, out_specs=P("node", SPACE), check_vma=False
    )
```

```python
import math

import jax
import jax.numpy as jnp
from jax import lax
from jax.experimental import pallas as pl
from jax.experimental.pallas import tpu as pltpu
from jax.sharding import Mesh, PartitionSpec as P

NY = 128
NZ = 64
ROWS = 128
SPLIT = (96, 32)
SPACE = ("z", "y", "core")


def ahead(values, offset):
    tail = jnp.zeros(values.shape[:-1] + (offset,), values.dtype)
    return jnp.concatenate([values[..., offset:], tail], axis=-1)


def behind(values, offset):
    head = jnp.zeros(values.shape[:-1] + (offset,), values.dtype)
    return jnp.concatenate([head, values[..., :-offset]], axis=-1)


def stencil_kernel(x_ref, below_ref, above_ref, coef_ref, out_ref):
    span = below_ref.shape[1]
    lane = lax.broadcasted_iota(jnp.int32, (1, span), 1)
    inner = lane < span - 2 * NZ
    planes = [x_ref[p].astype(jnp.float32) for p in range(2)]
    below = below_ref[...].astype(jnp.float32)
    above = above_ref[...].astype(jnp.float32)
    for p in range(2):
        v = planes[p]

        def coef(t):
            return coef_ref[t, p:p + 1, :]

        near = coef(0) * pltpu.roll(v, span - 1, 1)
        near = near + coef(1) * pltpu.roll(v, 1, 1)
        near = near + coef(2) * pltpu.roll(v, span - NZ, 1)
        near = near + coef(3) * pltpu.roll(v, NZ, 1)
        near = near + coef(4) * (below if p == 0 else planes[0])
        near = near + coef(5) * (planes[1] if p == 0 else above)
        total = coef(6) * v - near
        out_ref[p] = jnp.where(inner, total, 0.0).astype(out_ref.dtype)


def stencil(field, below, above, coef):
    planes, snaps, span = field.shape
    return pl.pallas_call(
        stencil_kernel,
        grid=(snaps // ROWS,),
        in_specs=[
            pl.BlockSpec((planes, ROWS, span), lambda i: (0, i, 0)),
            pl.BlockSpec((ROWS, span), lambda i: (i, 0)),
            pl.BlockSpec((ROWS, span), lambda i: (i, 0)),
            pl.BlockSpec(coef.shape, lambda i: (0, 0, 0)),
        ],
        out_specs=pl.BlockSpec((planes, ROWS, span), lambda i: (0, i, 0)),
        out_shape=jax.ShapeDtypeStruct(field.shape, jnp.bfloat16),
    )(field, below, above, coef)


def weights(kap_chunk, kap_below, kap_above):
    span = kap_chunk.shape[-1]
    kc = kap_chunk.astype(jnp.float32)
    zpos = jnp.arange(span, dtype=jnp.int32) % NZ
    k_zp = jnp.where(zpos != NZ - 1, jnp.roll(kc, -1, axis=-1), 0.0)
    k_zm = jnp.where(zpos != 0, jnp.roll(kc, 1, axis=-1), 0.0)
    k_xm = jnp.stack([kap_below.astype(jnp.float32), kc[0]])
    k_xp = jnp.stack([kc[1], kap_above.astype(jnp.float32)])
    near = [k_zp, k_zm, jnp.roll(kc, -NZ, axis=-1), jnp.roll(kc, NZ, axis=-1), k_xm, k_xp]
    zmask = [zpos != NZ - 1, zpos != 0, True, True, True, True]
    w = [0.5 * (kc + k) for k in near]
    diag = w[0] + w[1] + w[2] + w[3] + w[4] + w[5]
    return jnp.stack([jnp.where(m, wt, 0.0) for m, wt in zip(zmask, w)] + [diag])


def chunked(values, nodes):
    chunk = values.shape[-1] // nodes
    zero = jnp.zeros(values.shape[:-1] + (NZ,), values.dtype)
    pieces = []
    for q in range(nodes):
        after = values[..., (q + 1) * chunk:(q + 1) * chunk + NZ] if q + 1 < nodes else zero
        before = values[..., q * chunk - NZ:q * chunk] if q > 0 else zero
        pieces.append(jnp.concatenate([values[..., q * chunk:(q + 1) * chunk], after, before], axis=-1))
    return jnp.stack(pieces, axis=-3)


def per_device(snapshots, kappa):
    rows, planes, width = snapshots.shape
    nodes = lax.axis_size("node")
    sizes = [lax.axis_size(a) for a in SPACE]
    spaces = math.prod(sizes)
    me = lax.axis_index("node")
    chunk = width // nodes
    span = chunk + 2 * NZ
    snaps = rows * nodes

    up = [(i, i + 1) for i in range(spaces - 1)]
    down = [(j, i) for i, j in up]

    images, fields, fronts = [], [], []
    start = 0
    for g, step in enumerate(SPLIT):
        major = jnp.transpose(snapshots[start:start + step], (1, 0, 2))
        start += step
        field = lax.all_to_all(chunked(major, nodes), "node", 1, 1, tiled=True).reshape(planes, nodes * step, span)
        below = lax.ppermute(field[1], SPACE, up)
        above = lax.ppermute(field[0], SPACE, down)
        fields.append(field)
        fronts.append((below, above))
        if g == 0:
            late, _ = lax.optimization_barrier((kappa, field))
            kap_chunk = jnp.take(chunked(late[:, None], nodes)[:, :, 0], me, axis=1)
            kap_below = lax.ppermute(kap_chunk[1], SPACE, up)
            kap_above = lax.ppermute(kap_chunk[0], SPACE, down)
            coef = weights(kap_chunk, kap_below, kap_above)
    for field, (below, above) in zip(fields, fronts):
        images.append(stencil(field, below, above, coef))
    dims = (((0, 2), (0, 2)), ((), ()))
    part = jnp.concatenate([
        jnp.concatenate([
            lax.dot_general(im, fd, dims, preferred_element_type=jnp.float32)
            for fd in fields], axis=1)
        for im in images], axis=0)

    def in_order(values, axis):
        parts = []
        for a in range(nodes):
            for g, step in enumerate(SPLIT):
                first = nodes * sum(SPLIT[:g]) + a * step
                parts.append(lax.slice_in_dim(values, first, first + step, axis=axis))
        return jnp.concatenate(parts, axis=axis)

    part = in_order(in_order(part, 0), 1)
    part = part.reshape(nodes, rows, snaps)
    total = jnp.take(part, me, axis=0)
    for d in range(1, nodes):
        blk = jnp.take(part, (me + d) % nodes, axis=0)
        total = total + lax.ppermute(blk, "node", [(i, (i + d) % nodes) for i in range(nodes)])
    total = total.reshape((rows,) + tuple(sizes) + (snaps // spaces,))
    for axis in reversed(range(len(SPACE))):
        total = jnp.moveaxis(total, axis + 1, 0)
        total = lax.all_to_all(total, SPACE[axis], 0, 0, tiled=True).sum(axis=0)
    out = total

    scale = jnp.float32(1.0 / math.sqrt(planes * spaces * NY * NZ))
    return out * scale


def solution(mesh):
    node, space = mesh.devices.shape
    cores = 2
    fine = Mesh(mesh.devices.reshape(node, space // (4 * cores), 4, cores), ("node",) + SPACE)
    placed = (P("node", SPACE, None), P(SPACE, None))
    return jax.shard_map(
        per_device, mesh=fine, in_specs=placed, out_specs=P("node", SPACE), check_vma=False
    )
```

```python
import math

import jax
import jax.numpy as jnp
from jax import lax
from jax.experimental import pallas as pl
from jax.experimental.pallas import tpu as pltpu
from jax.sharding import Mesh, PartitionSpec as P

NY = 128
NZ = 64
ROWS = 128
GROUPS = 2
SPACE = ("z", "y", "core")


def ahead(values, offset):
    tail = jnp.zeros(values.shape[:-1] + (offset,), values.dtype)
    return jnp.concatenate([values[..., offset:], tail], axis=-1)


def behind(values, offset):
    head = jnp.zeros(values.shape[:-1] + (offset,), values.dtype)
    return jnp.concatenate([head, values[..., :-offset]], axis=-1)


def stencil_kernel(x_ref, below_ref, above_ref, coef_ref, out_ref):
    span = below_ref.shape[1]
    lane = lax.broadcasted_iota(jnp.int32, (1, span), 1)
    inner = lane < span - 2 * NZ
    planes = [x_ref[p].astype(jnp.float32) for p in range(2)]
    below = below_ref[...].astype(jnp.float32)
    above = above_ref[...].astype(jnp.float32)
    for p in range(2):
        v = planes[p]

        def coef(t):
            return coef_ref[t, p:p + 1, :]

        near = coef(0) * pltpu.roll(v, span - 1, 1)
        near = near + coef(1) * pltpu.roll(v, 1, 1)
        near = near + coef(2) * pltpu.roll(v, span - NZ, 1)
        near = near + coef(3) * pltpu.roll(v, NZ, 1)
        near = near + coef(4) * (below if p == 0 else planes[0])
        near = near + coef(5) * (planes[1] if p == 0 else above)
        total = coef(6) * v - near
        out_ref[p] = jnp.where(inner, total, 0.0).astype(out_ref.dtype)


def stencil(field, below, above, coef):
    planes, snaps, span = field.shape
    return pl.pallas_call(
        stencil_kernel,
        grid=(snaps // ROWS,),
        in_specs=[
            pl.BlockSpec((planes, ROWS, span), lambda i: (0, i, 0)),
            pl.BlockSpec((ROWS, span), lambda i: (i, 0)),
            pl.BlockSpec((ROWS, span), lambda i: (i, 0)),
            pl.BlockSpec(coef.shape, lambda i: (0, 0, 0)),
        ],
        out_specs=pl.BlockSpec((planes, ROWS, span), lambda i: (0, i, 0)),
        out_shape=jax.ShapeDtypeStruct(field.shape, jnp.bfloat16),
    )(field, below, above, coef)


def weights(kap_chunk, kap_below, kap_above):
    span = kap_chunk.shape[-1]
    kc = kap_chunk.astype(jnp.float32)
    zpos = jnp.arange(span, dtype=jnp.int32) % NZ
    k_zp = jnp.where(zpos != NZ - 1, jnp.roll(kc, -1, axis=-1), 0.0)
    k_zm = jnp.where(zpos != 0, jnp.roll(kc, 1, axis=-1), 0.0)
    k_xm = jnp.stack([kap_below.astype(jnp.float32), kc[0]])
    k_xp = jnp.stack([kc[1], kap_above.astype(jnp.float32)])
    near = [k_zp, k_zm, jnp.roll(kc, -NZ, axis=-1), jnp.roll(kc, NZ, axis=-1), k_xm, k_xp]
    zmask = [zpos != NZ - 1, zpos != 0, True, True, True, True]
    w = [0.5 * (kc + k) for k in near]
    diag = w[0] + w[1] + w[2] + w[3] + w[4] + w[5]
    return jnp.stack([jnp.where(m, wt, 0.0) for m, wt in zip(zmask, w)] + [diag])


def chunked(values, nodes):
    chunk = values.shape[-1] // nodes
    zero = jnp.zeros(values.shape[:-1] + (NZ,), values.dtype)
    pieces = []
    for q in range(nodes):
        after = values[..., (q + 1) * chunk:(q + 1) * chunk + NZ] if q + 1 < nodes else zero
        before = values[..., q * chunk - NZ:q * chunk] if q > 0 else zero
        pieces.append(jnp.concatenate([values[..., q * chunk:(q + 1) * chunk], after, before], axis=-1))
    return jnp.stack(pieces, axis=-3)


def per_device(snapshots, kappa):
    rows, planes, width = snapshots.shape
    nodes = lax.axis_size("node")
    sizes = [lax.axis_size(a) for a in SPACE]
    spaces = math.prod(sizes)
    me = lax.axis_index("node")
    chunk = width // nodes
    span = chunk + 2 * NZ
    snaps = rows * nodes

    up = [(i, i + 1) for i in range(spaces - 1)]
    down = [(j, i) for i, j in up]

    step = rows // GROUPS
    images, fields, fronts = [], [], []
    for g in range(GROUPS):
        major = jnp.transpose(snapshots[g * step:(g + 1) * step], (1, 0, 2))
        field = lax.all_to_all(chunked(major, nodes), "node", 1, 1, tiled=True).reshape(planes, nodes * step, span)
        below = lax.ppermute(field[1], SPACE, up)
        above = lax.ppermute(field[0], SPACE, down)
        fields.append(field)
        fronts.append((below, above))
        if g == 0:
            late, _ = lax.optimization_barrier((kappa, field))
            kap_chunk = jnp.take(chunked(late[:, None], nodes)[:, :, 0], me, axis=1)
            kap_below = lax.ppermute(kap_chunk[1], SPACE, up)
            kap_above = lax.ppermute(kap_chunk[0], SPACE, down)
            coef = weights(kap_chunk, kap_below, kap_above)
    for field, (below, above) in zip(fields, fronts):
        images.append(stencil(field, below, above, coef))
    dims = (((0, 2), (0, 2)), ((), ()))
    part = jnp.concatenate([
        jnp.concatenate([
            lax.dot_general(im, fd, dims, preferred_element_type=jnp.float32)
            for fd in fields], axis=1)
        for im in images], axis=0)
    part = part.reshape(GROUPS, nodes, step, snaps)
    total = jnp.take(part, me, axis=1)
    for d in range(1, nodes):
        blk = jnp.take(part, (me + d) % nodes, axis=1)
        total = total + lax.ppermute(blk, "node", [(i, (i + d) % nodes) for i in range(nodes)])
    total = total.reshape(rows, GROUPS, nodes, step).transpose(0, 2, 1, 3)
    total = total.reshape((rows,) + tuple(sizes) + (snaps // spaces,))
    total = jnp.moveaxis(total, 3, 0)
    total = lax.all_to_all(total, SPACE[2], 0, 0, tiled=True).sum(axis=0)
    total = total.reshape(rows, sizes[0] * sizes[1], snaps // spaces)
    total = jnp.moveaxis(total, 1, 0)
    total = lax.all_to_all(total, SPACE[:2], 0, 0, tiled=True).sum(axis=0)
    out = total

    scale = jnp.float32(1.0 / math.sqrt(planes * spaces * NY * NZ))
    return out * scale


def solution(mesh):
    node, space = mesh.devices.shape
    cores = 2
    fine = Mesh(mesh.devices.reshape(node, space // (4 * cores), 4, cores), ("node",) + SPACE)
    placed = (P("node", SPACE, None), P(SPACE, None))
    return jax.shard_map(
        per_device, mesh=fine, in_specs=placed, out_specs=P("node", SPACE), check_vma=False
    )
```

```python
import math

import jax
import jax.numpy as jnp
from jax import lax
from jax.experimental import pallas as pl
from jax.experimental.pallas import tpu as pltpu
from jax.sharding import Mesh, PartitionSpec as P

NY = 128
NZ = 64
ROWS = 128
GROUPS = 2
SPACE = ("z", "y", "core")


def ahead(values, offset):
    tail = jnp.zeros(values.shape[:-1] + (offset,), values.dtype)
    return jnp.concatenate([values[..., offset:], tail], axis=-1)


def behind(values, offset):
    head = jnp.zeros(values.shape[:-1] + (offset,), values.dtype)
    return jnp.concatenate([head, values[..., :-offset]], axis=-1)


def stencil_kernel(x_ref, below_ref, above_ref, coef_ref, out_ref):
    span = below_ref.shape[1]
    lane = lax.broadcasted_iota(jnp.int32, (1, span), 1)
    inner = lane < span - 2 * NZ
    planes = [x_ref[p].astype(jnp.float32) for p in range(2)]
    below = below_ref[...].astype(jnp.float32)
    above = above_ref[...].astype(jnp.float32)
    for p in range(2):
        v = planes[p]

        def coef(t):
            return coef_ref[t, p:p + 1, :]

        near = coef(0) * pltpu.roll(v, span - 1, 1)
        near = near + coef(1) * pltpu.roll(v, 1, 1)
        near = near + coef(2) * pltpu.roll(v, span - NZ, 1)
        near = near + coef(3) * pltpu.roll(v, NZ, 1)
        near = near + coef(4) * (below if p == 0 else planes[0])
        near = near + coef(5) * (planes[1] if p == 0 else above)
        total = coef(6) * v - near
        out_ref[p] = jnp.where(inner, total, 0.0).astype(out_ref.dtype)


def stencil(field, below, above, coef):
    planes, snaps, span = field.shape
    return pl.pallas_call(
        stencil_kernel,
        grid=(snaps // ROWS,),
        in_specs=[
            pl.BlockSpec((planes, ROWS, span), lambda i: (0, i, 0)),
            pl.BlockSpec((ROWS, span), lambda i: (i, 0)),
            pl.BlockSpec((ROWS, span), lambda i: (i, 0)),
            pl.BlockSpec(coef.shape, lambda i: (0, 0, 0)),
        ],
        out_specs=pl.BlockSpec((planes, ROWS, span), lambda i: (0, i, 0)),
        out_shape=jax.ShapeDtypeStruct(field.shape, jnp.bfloat16),
    )(field, below, above, coef)


def weights(kap_chunk, kap_below, kap_above):
    span = kap_chunk.shape[-1]
    kc = kap_chunk.astype(jnp.float32)
    zpos = jnp.arange(span, dtype=jnp.int32) % NZ
    k_zp = jnp.where(zpos != NZ - 1, jnp.roll(kc, -1, axis=-1), 0.0)
    k_zm = jnp.where(zpos != 0, jnp.roll(kc, 1, axis=-1), 0.0)
    k_xm = jnp.stack([kap_below.astype(jnp.float32), kc[0]])
    k_xp = jnp.stack([kc[1], kap_above.astype(jnp.float32)])
    near = [k_zp, k_zm, jnp.roll(kc, -NZ, axis=-1), jnp.roll(kc, NZ, axis=-1), k_xm, k_xp]
    zmask = [zpos != NZ - 1, zpos != 0, True, True, True, True]
    w = [0.5 * (kc + k) for k in near]
    diag = w[0] + w[1] + w[2] + w[3] + w[4] + w[5]
    return jnp.stack([jnp.where(m, wt, 0.0) for m, wt in zip(zmask, w)] + [diag])


def chunked(values, nodes):
    chunk = values.shape[-1] // nodes
    zero = jnp.zeros(values.shape[:-1] + (NZ,), values.dtype)
    pieces = []
    for q in range(nodes):
        after = values[..., (q + 1) * chunk:(q + 1) * chunk + NZ] if q + 1 < nodes else zero
        before = values[..., q * chunk - NZ:q * chunk] if q > 0 else zero
        pieces.append(jnp.concatenate([values[..., q * chunk:(q + 1) * chunk], after, before], axis=-1))
    return jnp.stack(pieces, axis=-3)


def per_device(snapshots, kappa):
    rows, planes, width = snapshots.shape
    nodes = lax.axis_size("node")
    sizes = [lax.axis_size(a) for a in SPACE]
    spaces = math.prod(sizes)
    me = lax.axis_index("node")
    chunk = width // nodes
    span = chunk + 2 * NZ
    snaps = rows * nodes

    up = [(i, i + 1) for i in range(spaces - 1)]
    down = [(j, i) for i, j in up]

    step = rows // GROUPS
    images, fields, fronts = [], [], []
    for g in range(GROUPS):
        major = jnp.transpose(snapshots[g * step:(g + 1) * step], (1, 0, 2))
        field = lax.all_to_all(chunked(major, nodes), "node", 1, 1, tiled=True).reshape(planes, nodes * step, span)
        below = lax.ppermute(field[1], SPACE, up)
        above = lax.ppermute(field[0], SPACE, down)
        fields.append(field)
        fronts.append((below, above))
        if g == 0:
            late, _ = lax.optimization_barrier((kappa, field))
            kap_chunk = jnp.take(chunked(late[:, None], nodes)[:, :, 0], me, axis=1)
            kap_below = lax.ppermute(kap_chunk[1], SPACE, up)
            kap_above = lax.ppermute(kap_chunk[0], SPACE, down)
            coef = weights(kap_chunk, kap_below, kap_above)
    for field, (below, above) in zip(fields, fronts):
        images.append(stencil(field, below, above, coef))
    dims = (((0, 2), (0, 2)), ((), ()))
    part = jnp.concatenate([
        jnp.concatenate([
            lax.dot_general(im, fd, dims, preferred_element_type=jnp.float32)
            for fd in fields], axis=1)
        for im in images], axis=0)
    part = part.reshape(GROUPS, nodes, step, snaps)
    total = jnp.take(part, me, axis=1)
    for d in range(1, nodes):
        blk = jnp.take(part, (me + d) % nodes, axis=1)
        total = total + lax.ppermute(blk, "node", [(i, (i + d) % nodes) for i in range(nodes)])
    total = total.reshape(rows, GROUPS, nodes, step).transpose(0, 2, 1, 3)
    total = total.reshape((rows,) + tuple(sizes) + (snaps // spaces,))
    total = total.reshape(rows, spaces, snaps // spaces)
    total = jnp.moveaxis(total, 1, 0)
    total = lax.all_to_all(total, SPACE, 0, 0, tiled=True).sum(axis=0)
    out = total

    scale = jnp.float32(1.0 / math.sqrt(planes * spaces * NY * NZ))
    return out * scale


def solution(mesh):
    node, space = mesh.devices.shape
    cores = 2
    fine = Mesh(mesh.devices.reshape(node, space // (4 * cores), 4, cores), ("node",) + SPACE)
    placed = (P("node", SPACE, None), P(SPACE, None))
    return jax.shard_map(
        per_device, mesh=fine, in_specs=placed, out_specs=P("node", SPACE), check_vma=False
    )
```

```python
import math

import jax
import jax.numpy as jnp
from jax import lax
from jax.experimental import pallas as pl
from jax.experimental.pallas import tpu as pltpu
from jax.sharding import Mesh, PartitionSpec as P

NY = 128
NZ = 64
ROWS = 128
GROUPS = 2
SPACE = ("z", "y", "core")


def ahead(values, offset):
    tail = jnp.zeros(values.shape[:-1] + (offset,), values.dtype)
    return jnp.concatenate([values[..., offset:], tail], axis=-1)


def behind(values, offset):
    head = jnp.zeros(values.shape[:-1] + (offset,), values.dtype)
    return jnp.concatenate([head, values[..., :-offset]], axis=-1)


def stencil_kernel(x_ref, below_ref, above_ref, coef_ref, out_ref):
    span = below_ref.shape[1]
    lane = lax.broadcasted_iota(jnp.int32, (1, span), 1)
    inner = lane < span - 2 * NZ
    planes = [x_ref[p].astype(jnp.float32) for p in range(2)]
    below = below_ref[...].astype(jnp.float32)
    above = above_ref[...].astype(jnp.float32)
    for p in range(2):
        v = planes[p]

        def coef(t):
            return coef_ref[t, p:p + 1, :]

        near = coef(0) * pltpu.roll(v, span - 1, 1)
        near = near + coef(1) * pltpu.roll(v, 1, 1)
        near = near + coef(2) * pltpu.roll(v, span - NZ, 1)
        near = near + coef(3) * pltpu.roll(v, NZ, 1)
        near = near + coef(4) * (below if p == 0 else planes[0])
        near = near + coef(5) * (planes[1] if p == 0 else above)
        total = coef(6) * v - near
        out_ref[p] = jnp.where(inner, total, 0.0).astype(out_ref.dtype)


def stencil(field, below, above, coef):
    planes, snaps, span = field.shape
    return pl.pallas_call(
        stencil_kernel,
        grid=(snaps // ROWS,),
        in_specs=[
            pl.BlockSpec((planes, ROWS, span), lambda i: (0, i, 0)),
            pl.BlockSpec((ROWS, span), lambda i: (i, 0)),
            pl.BlockSpec((ROWS, span), lambda i: (i, 0)),
            pl.BlockSpec(coef.shape, lambda i: (0, 0, 0)),
        ],
        out_specs=pl.BlockSpec((planes, ROWS, span), lambda i: (0, i, 0)),
        out_shape=jax.ShapeDtypeStruct(field.shape, jnp.bfloat16),
    )(field, below, above, coef)


def weights(kap_chunk, kap_below, kap_above):
    span = kap_chunk.shape[-1]
    kc = kap_chunk.astype(jnp.float32)
    zpos = jnp.arange(span, dtype=jnp.int32) % NZ
    k_zp = jnp.where(zpos != NZ - 1, jnp.roll(kc, -1, axis=-1), 0.0)
    k_zm = jnp.where(zpos != 0, jnp.roll(kc, 1, axis=-1), 0.0)
    k_xm = jnp.stack([kap_below.astype(jnp.float32), kc[0]])
    k_xp = jnp.stack([kc[1], kap_above.astype(jnp.float32)])
    near = [k_zp, k_zm, jnp.roll(kc, -NZ, axis=-1), jnp.roll(kc, NZ, axis=-1), k_xm, k_xp]
    zmask = [zpos != NZ - 1, zpos != 0, True, True, True, True]
    w = [0.5 * (kc + k) for k in near]
    diag = w[0] + w[1] + w[2] + w[3] + w[4] + w[5]
    return jnp.stack([jnp.where(m, wt, 0.0) for m, wt in zip(zmask, w)] + [diag])


def chunked(values, nodes):
    chunk = values.shape[-1] // nodes
    zero = jnp.zeros(values.shape[:-1] + (NZ,), values.dtype)
    pieces = []
    for q in range(nodes):
        after = values[..., (q + 1) * chunk:(q + 1) * chunk + NZ] if q + 1 < nodes else zero
        before = values[..., q * chunk - NZ:q * chunk] if q > 0 else zero
        pieces.append(jnp.concatenate([values[..., q * chunk:(q + 1) * chunk], after, before], axis=-1))
    return jnp.stack(pieces, axis=-3)


def per_device(snapshots, kappa):
    rows, planes, width = snapshots.shape
    nodes = lax.axis_size("node")
    sizes = [lax.axis_size(a) for a in SPACE]
    spaces = math.prod(sizes)
    me = lax.axis_index("node")
    chunk = width // nodes
    span = chunk + 2 * NZ
    snaps = rows * nodes

    up = [(i, i + 1) for i in range(spaces - 1)]
    down = [(j, i) for i, j in up]

    step = rows // GROUPS
    images, fields, fronts = [], [], []
    for g in range(GROUPS):
        major = jnp.transpose(snapshots[g * step:(g + 1) * step], (1, 0, 2))
        field = lax.all_to_all(chunked(major, nodes), "node", 1, 1, tiled=True).reshape(planes, nodes * step, span)
        below = lax.ppermute(field[1], SPACE, up)
        above = lax.ppermute(field[0], SPACE, down)
        fields.append(field)
        fronts.append((below, above))
        if g == 0:
            late, _ = lax.optimization_barrier((kappa, field))
            kap_chunk = jnp.take(chunked(late[:, None], nodes)[:, :, 0], me, axis=1)
            kap_below = lax.ppermute(kap_chunk[1], SPACE, up)
            kap_above = lax.ppermute(kap_chunk[0], SPACE, down)
            coef = weights(kap_chunk, kap_below, kap_above)
    for field, (below, above) in zip(fields, fronts):
        images.append(stencil(field, below, above, coef))
    dims = (((0, 2), (0, 2)), ((), ()))
    part = jnp.concatenate([
        jnp.concatenate([
            lax.dot_general(im, fd, dims, preferred_element_type=jnp.float32)
            for fd in fields], axis=1)
        for im in images], axis=0)
    part = part.reshape(GROUPS, nodes, step, GROUPS, nodes, step).transpose(1, 0, 2, 4, 3, 5)
    part = part.reshape((nodes, rows) + tuple(sizes) + (snaps // spaces,))
    part = jnp.moveaxis(part, 4, 1).reshape(nodes * sizes[2], rows, -1)
    total = lax.all_to_all(part, ("node", SPACE[2]), 0, 0, tiled=True).sum(axis=0)
    total = total.reshape(rows, sizes[0] * sizes[1], snaps // spaces)
    total = jnp.moveaxis(total, 1, 0)
    total = lax.all_to_all(total, SPACE[:2], 0, 0, tiled=True).sum(axis=0)
    out = total

    scale = jnp.float32(1.0 / math.sqrt(planes * spaces * NY * NZ))
    return out * scale


def solution(mesh):
    node, space = mesh.devices.shape
    cores = 2
    fine = Mesh(mesh.devices.reshape(node, space // (4 * cores), 4, cores), ("node",) + SPACE)
    placed = (P("node", SPACE, None), P(SPACE, None))
    return jax.shard_map(
        per_device, mesh=fine, in_specs=placed, out_specs=P("node", SPACE), check_vma=False
    )
```

```python
import math

import jax
import jax.numpy as jnp
from jax import lax
from jax.experimental import pallas as pl
from jax.experimental.pallas import tpu as pltpu
from jax.sharding import Mesh, PartitionSpec as P

NY = 128
NZ = 64
ROWS = 128
GROUPS = 2
SPACE = ("z", "y", "core")


def ahead(values, offset):
    tail = jnp.zeros(values.shape[:-1] + (offset,), values.dtype)
    return jnp.concatenate([values[..., offset:], tail], axis=-1)


def behind(values, offset):
    head = jnp.zeros(values.shape[:-1] + (offset,), values.dtype)
    return jnp.concatenate([head, values[..., :-offset]], axis=-1)


def stencil_kernel(x_ref, below_ref, above_ref, coef_ref, out_ref):
    span = below_ref.shape[1]
    lane = lax.broadcasted_iota(jnp.int32, (1, span), 1)
    inner = lane < span - 2 * NZ
    planes = [x_ref[p].astype(jnp.float32) for p in range(2)]
    below = below_ref[...].astype(jnp.float32)
    above = above_ref[...].astype(jnp.float32)
    for p in range(2):
        v = planes[p]

        def coef(t):
            return coef_ref[t, p:p + 1, :]

        near = coef(0) * pltpu.roll(v, span - 1, 1)
        near = near + coef(1) * pltpu.roll(v, 1, 1)
        near = near + coef(2) * pltpu.roll(v, span - NZ, 1)
        near = near + coef(3) * pltpu.roll(v, NZ, 1)
        near = near + coef(4) * (below if p == 0 else planes[0])
        near = near + coef(5) * (planes[1] if p == 0 else above)
        total = coef(6) * v - near
        out_ref[p] = jnp.where(inner, total, 0.0).astype(out_ref.dtype)


def stencil(field, below, above, coef):
    planes, snaps, span = field.shape
    return pl.pallas_call(
        stencil_kernel,
        grid=(snaps // ROWS,),
        in_specs=[
            pl.BlockSpec((planes, ROWS, span), lambda i: (0, i, 0)),
            pl.BlockSpec((ROWS, span), lambda i: (i, 0)),
            pl.BlockSpec((ROWS, span), lambda i: (i, 0)),
            pl.BlockSpec(coef.shape, lambda i: (0, 0, 0)),
        ],
        out_specs=pl.BlockSpec((planes, ROWS, span), lambda i: (0, i, 0)),
        out_shape=jax.ShapeDtypeStruct(field.shape, jnp.bfloat16),
    )(field, below, above, coef)


def weights(kap_chunk, kap_below, kap_above):
    span = kap_chunk.shape[-1]
    kc = kap_chunk.astype(jnp.float32)
    zpos = jnp.arange(span, dtype=jnp.int32) % NZ
    k_zp = jnp.where(zpos != NZ - 1, jnp.roll(kc, -1, axis=-1), 0.0)
    k_zm = jnp.where(zpos != 0, jnp.roll(kc, 1, axis=-1), 0.0)
    k_xm = jnp.stack([kap_below.astype(jnp.float32), kc[0]])
    k_xp = jnp.stack([kc[1], kap_above.astype(jnp.float32)])
    near = [k_zp, k_zm, jnp.roll(kc, -NZ, axis=-1), jnp.roll(kc, NZ, axis=-1), k_xm, k_xp]
    zmask = [zpos != NZ - 1, zpos != 0, True, True, True, True]
    w = [0.5 * (kc + k) for k in near]
    diag = w[0] + w[1] + w[2] + w[3] + w[4] + w[5]
    return jnp.stack([jnp.where(m, wt, 0.0) for m, wt in zip(zmask, w)] + [diag])


def chunked(values, nodes):
    chunk = values.shape[-1] // nodes
    zero = jnp.zeros(values.shape[:-1] + (NZ,), values.dtype)
    pieces = []
    for q in range(nodes):
        after = values[..., (q + 1) * chunk:(q + 1) * chunk + NZ] if q + 1 < nodes else zero
        before = values[..., q * chunk - NZ:q * chunk] if q > 0 else zero
        pieces.append(jnp.concatenate([values[..., q * chunk:(q + 1) * chunk], after, before], axis=-1))
    return jnp.stack(pieces, axis=-3)


def per_device(snapshots, kappa):
    rows, planes, width = snapshots.shape
    nodes = lax.axis_size("node")
    sizes = [lax.axis_size(a) for a in SPACE]
    spaces = math.prod(sizes)
    me = lax.axis_index("node")
    chunk = width // nodes
    span = chunk + 2 * NZ
    snaps = rows * nodes

    up = [(i, i + 1) for i in range(spaces - 1)]
    down = [(j, i) for i, j in up]

    step = rows // GROUPS
    images, fields, fronts = [], [], []
    for g in range(GROUPS):
        major = jnp.transpose(snapshots[g * step:(g + 1) * step], (1, 0, 2))
        field = lax.all_to_all(chunked(major, nodes), "node", 1, 1, tiled=True).reshape(planes, nodes * step, span)
        below = lax.ppermute(field[1], SPACE, up)
        above = lax.ppermute(field[0], SPACE, down)
        fields.append(field)
        fronts.append((below, above))
        if g == 0:
            late, _ = lax.optimization_barrier((kappa, field))
            kap_chunk = jnp.take(chunked(late[:, None], nodes)[:, :, 0], me, axis=1)
            kap_below = lax.ppermute(kap_chunk[1], SPACE, up)
            kap_above = lax.ppermute(kap_chunk[0], SPACE, down)
            coef = weights(kap_chunk, kap_below, kap_above)
    for field, (below, above) in zip(fields, fronts):
        images.append(stencil(field, below, above, coef))
    dims = (((0, 2), (0, 2)), ((), ()))
    part = jnp.concatenate([
        jnp.concatenate([
            lax.dot_general(im, fd, dims, preferred_element_type=jnp.float32)
            for fd in fields], axis=1)
        for im in images], axis=0)
    cols = (GROUPS, nodes, sizes[0] // (GROUPS * nodes), sizes[1], sizes[2], snaps // spaces)
    part = jnp.moveaxis(part.reshape((snaps,) + cols), 5, 0)
    part = lax.all_to_all(part, SPACE[2], 0, 0, tiled=True).sum(axis=0)
    part = part.reshape(GROUPS, nodes, step, -1)
    total = jnp.take(part, me, axis=1)
    for d in range(1, nodes):
        blk = jnp.take(part, (me + d) % nodes, axis=1)
        total = total + lax.ppermute(blk, "node", [(i, (i + d) % nodes) for i in range(nodes)])
    total = total.reshape((rows,) + cols[:4] + cols[5:]).transpose(0, 2, 1, 3, 4, 5)
    total = total.reshape(rows, sizes[0] * sizes[1], snaps // spaces)
    total = jnp.moveaxis(total, 1, 0)
    total = lax.all_to_all(total, SPACE[:2], 0, 0, tiled=True).sum(axis=0)
    out = total

    scale = jnp.float32(1.0 / math.sqrt(planes * spaces * NY * NZ))
    return out * scale


def solution(mesh):
    node, space = mesh.devices.shape
    cores = 2
    fine = Mesh(mesh.devices.reshape(node, space // (4 * cores), 4, cores), ("node",) + SPACE)
    placed = (P("node", SPACE, None), P(SPACE, None))
    return jax.shard_map(
        per_device, mesh=fine, in_specs=placed, out_specs=P("node", SPACE), check_vma=False
    )
```

```python
import math

import jax
import jax.numpy as jnp
from jax import lax
from jax.experimental import pallas as pl
from jax.experimental.pallas import tpu as pltpu
from jax.sharding import Mesh, PartitionSpec as P

NY = 128
NZ = 64
ROWS = 128
GROUPS = 2
SPACE = ("z", "y", "core")


def ahead(values, offset):
    tail = jnp.zeros(values.shape[:-1] + (offset,), values.dtype)
    return jnp.concatenate([values[..., offset:], tail], axis=-1)


def behind(values, offset):
    head = jnp.zeros(values.shape[:-1] + (offset,), values.dtype)
    return jnp.concatenate([head, values[..., :-offset]], axis=-1)


def stencil_kernel(x_ref, below_ref, above_ref, coef_ref, out_ref):
    span = below_ref.shape[1]
    lane = lax.broadcasted_iota(jnp.int32, (1, span), 1)
    inner = lane < span - 2 * NZ
    planes = [x_ref[p].astype(jnp.float32) for p in range(2)]
    below = below_ref[...].astype(jnp.float32)
    above = above_ref[...].astype(jnp.float32)
    for p in range(2):
        v = planes[p]

        def coef(t):
            return coef_ref[t, p:p + 1, :]

        near = coef(0) * pltpu.roll(v, span - 1, 1)
        near = near + coef(1) * pltpu.roll(v, 1, 1)
        near = near + coef(2) * pltpu.roll(v, span - NZ, 1)
        near = near + coef(3) * pltpu.roll(v, NZ, 1)
        near = near + coef(4) * (below if p == 0 else planes[0])
        near = near + coef(5) * (planes[1] if p == 0 else above)
        total = coef(6) * v - near
        out_ref[p] = jnp.where(inner, total, 0.0).astype(out_ref.dtype)


def stencil(field, below, above, coef):
    planes, snaps, span = field.shape
    return pl.pallas_call(
        stencil_kernel,
        grid=(snaps // ROWS,),
        in_specs=[
            pl.BlockSpec((planes, ROWS, span), lambda i: (0, i, 0)),
            pl.BlockSpec((ROWS, span), lambda i: (i, 0)),
            pl.BlockSpec((ROWS, span), lambda i: (i, 0)),
            pl.BlockSpec(coef.shape, lambda i: (0, 0, 0)),
        ],
        out_specs=pl.BlockSpec((planes, ROWS, span), lambda i: (0, i, 0)),
        out_shape=jax.ShapeDtypeStruct(field.shape, jnp.bfloat16),
    )(field, below, above, coef)


def weights(kap_chunk, kap_below, kap_above):
    span = kap_chunk.shape[-1]
    kc = kap_chunk.astype(jnp.float32)
    zpos = jnp.arange(span, dtype=jnp.int32) % NZ
    k_zp = jnp.where(zpos != NZ - 1, jnp.roll(kc, -1, axis=-1), 0.0)
    k_zm = jnp.where(zpos != 0, jnp.roll(kc, 1, axis=-1), 0.0)
    k_xm = jnp.stack([kap_below.astype(jnp.float32), kc[0]])
    k_xp = jnp.stack([kc[1], kap_above.astype(jnp.float32)])
    near = [k_zp, k_zm, jnp.roll(kc, -NZ, axis=-1), jnp.roll(kc, NZ, axis=-1), k_xm, k_xp]
    zmask = [zpos != NZ - 1, zpos != 0, True, True, True, True]
    w = [0.5 * (kc + k) for k in near]
    diag = w[0] + w[1] + w[2] + w[3] + w[4] + w[5]
    return jnp.stack([jnp.where(m, wt, 0.0) for m, wt in zip(zmask, w)] + [diag])


def chunked(values, nodes):
    chunk = values.shape[-1] // nodes
    zero = jnp.zeros(values.shape[:-1] + (NZ,), values.dtype)
    pieces = []
    for q in range(nodes):
        after = values[..., (q + 1) * chunk:(q + 1) * chunk + NZ] if q + 1 < nodes else zero
        before = values[..., q * chunk - NZ:q * chunk] if q > 0 else zero
        pieces.append(jnp.concatenate([values[..., q * chunk:(q + 1) * chunk], after, before], axis=-1))
    return jnp.stack(pieces, axis=-3)


def per_device(snapshots, kappa):
    rows, planes, width = snapshots.shape
    nodes = lax.axis_size("node")
    sizes = [lax.axis_size(a) for a in SPACE]
    spaces = math.prod(sizes)
    me = lax.axis_index("node")
    chunk = width // nodes
    span = chunk + 2 * NZ
    snaps = rows * nodes

    up = [(i, i + 1) for i in range(spaces - 1)]
    down = [(j, i) for i, j in up]

    step = rows // GROUPS
    images, fields, fronts = [], [], []
    for g in range(GROUPS):
        major = jnp.transpose(snapshots[g * step:(g + 1) * step], (1, 0, 2))
        field = lax.all_to_all(chunked(major, nodes), "node", 1, 1, tiled=True).reshape(planes, nodes * step, span)
        below = lax.ppermute(field[1], SPACE, up)
        above = lax.ppermute(field[0], SPACE, down)
        fields.append(field)
        fronts.append((below, above))
        if g == 0:
            late, _ = lax.optimization_barrier((kappa, field))
            kap_chunk = jnp.take(chunked(late[:, None], nodes)[:, :, 0], me, axis=1)
            kap_below = lax.ppermute(kap_chunk[1], SPACE, up)
            kap_above = lax.ppermute(kap_chunk[0], SPACE, down)
            coef = weights(kap_chunk, kap_below, kap_above)
    for field, (below, above) in zip(fields, fronts):
        images.append(stencil(field, below, above, coef))
    dims = (((0, 2), (0, 2)), ((), ()))
    part = lax.dot_general(jnp.concatenate(images, axis=1), jnp.concatenate(fields, axis=1), dims,
                           preferred_element_type=jnp.float32)
    part = part.reshape(GROUPS, nodes, step, snaps)
    total = jnp.take(part, me, axis=1)
    for d in range(1, nodes):
        blk = jnp.take(part, (me + d) % nodes, axis=1)
        total = total + lax.ppermute(blk, "node", [(i, (i + d) % nodes) for i in range(nodes)])
    total = total.reshape(rows, GROUPS, nodes, step).transpose(0, 2, 1, 3)
    total = total.reshape((rows,) + tuple(sizes) + (snaps // spaces,))
    total = jnp.moveaxis(total, 3, 0)
    total = lax.all_to_all(total, SPACE[2], 0, 0, tiled=True).sum(axis=0)
    total = total.reshape(rows, sizes[0] * sizes[1], snaps // spaces)
    total = jnp.moveaxis(total, 1, 0)
    total = lax.all_to_all(total, SPACE[:2], 0, 0, tiled=True).sum(axis=0)
    out = total

    scale = jnp.float32(1.0 / math.sqrt(planes * spaces * NY * NZ))
    return out * scale


def solution(mesh):
    node, space = mesh.devices.shape
    cores = 2
    fine = Mesh(mesh.devices.reshape(node, space // (4 * cores), 4, cores), ("node",) + SPACE)
    placed = (P("node", SPACE, None), P(SPACE, None))
    return jax.shard_map(
        per_device, mesh=fine, in_specs=placed, out_specs=P("node", SPACE), check_vma=False
    )
```

```python
import math

import jax
import jax.numpy as jnp
from jax import lax
from jax.experimental import pallas as pl
from jax.experimental.pallas import tpu as pltpu
from jax.sharding import Mesh, PartitionSpec as P

NY = 128
NZ = 64
ROWS = 128
GROUPS = 2
SPACE = ("z", "y", "core")


def ahead(values, offset):
    tail = jnp.zeros(values.shape[:-1] + (offset,), values.dtype)
    return jnp.concatenate([values[..., offset:], tail], axis=-1)


def behind(values, offset):
    head = jnp.zeros(values.shape[:-1] + (offset,), values.dtype)
    return jnp.concatenate([head, values[..., :-offset]], axis=-1)


def stencil_kernel(x_ref, below_ref, above_ref, coef_ref, out_ref):
    span = below_ref.shape[1]
    lane = lax.broadcasted_iota(jnp.int32, (1, span), 1)
    inner = lane < span - 2 * NZ
    planes = [x_ref[p].astype(jnp.float32) for p in range(2)]
    below = below_ref[...].astype(jnp.float32)
    above = above_ref[...].astype(jnp.float32)
    for p in range(2):
        v = planes[p]

        def coef(t):
            return coef_ref[t, p:p + 1, :]

        near = coef(0) * pltpu.roll(v, span - 1, 1)
        near = near + coef(1) * pltpu.roll(v, 1, 1)
        near = near + coef(2) * pltpu.roll(v, span - NZ, 1)
        near = near + coef(3) * pltpu.roll(v, NZ, 1)
        near = near + coef(4) * (below if p == 0 else planes[0])
        near = near + coef(5) * (planes[1] if p == 0 else above)
        total = coef(6) * v - near
        out_ref[p] = jnp.where(inner, total, 0.0).astype(out_ref.dtype)


def stencil(field, below, above, coef):
    planes, snaps, span = field.shape
    return pl.pallas_call(
        stencil_kernel,
        grid=(snaps // ROWS,),
        in_specs=[
            pl.BlockSpec((planes, ROWS, span), lambda i: (0, i, 0)),
            pl.BlockSpec((ROWS, span), lambda i: (i, 0)),
            pl.BlockSpec((ROWS, span), lambda i: (i, 0)),
            pl.BlockSpec(coef.shape, lambda i: (0, 0, 0)),
        ],
        out_specs=pl.BlockSpec((planes, ROWS, span), lambda i: (0, i, 0)),
        out_shape=jax.ShapeDtypeStruct(field.shape, jnp.bfloat16),
    )(field, below, above, coef)


def weights(kap_chunk, kap_below, kap_above):
    span = kap_chunk.shape[-1]
    kc = kap_chunk.astype(jnp.float32)
    zpos = jnp.arange(span, dtype=jnp.int32) % NZ
    k_zp = jnp.where(zpos != NZ - 1, jnp.roll(kc, -1, axis=-1), 0.0)
    k_zm = jnp.where(zpos != 0, jnp.roll(kc, 1, axis=-1), 0.0)
    k_xm = jnp.stack([kap_below.astype(jnp.float32), kc[0]])
    k_xp = jnp.stack([kc[1], kap_above.astype(jnp.float32)])
    near = [k_zp, k_zm, jnp.roll(kc, -NZ, axis=-1), jnp.roll(kc, NZ, axis=-1), k_xm, k_xp]
    zmask = [zpos != NZ - 1, zpos != 0, True, True, True, True]
    w = [0.5 * (kc + k) for k in near]
    diag = w[0] + w[1] + w[2] + w[3] + w[4] + w[5]
    return jnp.stack([jnp.where(m, wt, 0.0) for m, wt in zip(zmask, w)] + [diag])


def chunked(values, nodes):
    chunk = values.shape[-1] // nodes
    zero = jnp.zeros(values.shape[:-1] + (NZ,), values.dtype)
    pieces = []
    for q in range(nodes):
        after = values[..., (q + 1) * chunk:(q + 1) * chunk + NZ] if q + 1 < nodes else zero
        before = values[..., q * chunk - NZ:q * chunk] if q > 0 else zero
        pieces.append(jnp.concatenate([values[..., q * chunk:(q + 1) * chunk], after, before], axis=-1))
    return jnp.stack(pieces, axis=-3)


def per_device(snapshots, kappa):
    rows, planes, width = snapshots.shape
    nodes = lax.axis_size("node")
    sizes = [lax.axis_size(a) for a in SPACE]
    spaces = math.prod(sizes)
    me = lax.axis_index("node")
    chunk = width // nodes
    span = chunk + 2 * NZ
    snaps = rows * nodes

    up = [(i, i + 1) for i in range(spaces - 1)]
    down = [(j, i) for i, j in up]

    step = rows // GROUPS
    images, fields, fronts = [], [], []
    for g in range(GROUPS):
        major = jnp.transpose(snapshots[g * step:(g + 1) * step], (1, 0, 2))
        field = lax.all_to_all(chunked(major, nodes), "node", 1, 1, tiled=True).reshape(planes, nodes * step, span)
        below = lax.ppermute(field[1], SPACE, up)
        above = lax.ppermute(field[0], SPACE, down)
        fields.append(field)
        fronts.append((below, above))
        if g == 0:
            late, _ = lax.optimization_barrier((kappa, field))
            kap_chunk = jnp.take(chunked(late[:, None], nodes)[:, :, 0], me, axis=1)
            kap_below = lax.ppermute(kap_chunk[1], SPACE, up)
            kap_above = lax.ppermute(kap_chunk[0], SPACE, down)
            coef = weights(kap_chunk, kap_below, kap_above)
    for field, (below, above) in zip(fields, fronts):
        images.append(stencil(field, below, above, coef))
    dims = (((0, 2), (0, 2)), ((), ()))
    part = jnp.concatenate([
        jnp.concatenate([
            lax.dot_general(im, fd, dims, preferred_element_type=jnp.float32)
            for fd in fields], axis=1)
        for im in images], axis=0)
    part = part.reshape(GROUPS, nodes, step, snaps)
    total = jnp.take(part, me, axis=1)
    for d in range(1, nodes):
        blk = jnp.take(part, (me + d) % nodes, axis=1)
        total = total + lax.ppermute(blk, "node", [(i, (i + d) % nodes) for i in range(nodes)])
    total = total.reshape(rows, GROUPS, nodes, step).transpose(0, 2, 1, 3)
    total = total.reshape((rows,) + tuple(sizes) + (snaps // spaces,))
    core = lax.axis_index(SPACE[2])
    give = jnp.take(total, 1 - core, axis=3)
    total = jnp.take(total, core, axis=3) + lax.ppermute(give, SPACE[2], [(0, 1), (1, 0)])
    total = total.reshape(rows, sizes[0] * sizes[1], snaps // spaces)
    total = jnp.moveaxis(total, 1, 0)
    total = lax.all_to_all(total, SPACE[:2], 0, 0, tiled=True).sum(axis=0)
    out = total

    scale = jnp.float32(1.0 / math.sqrt(planes * spaces * NY * NZ))
    return out * scale


def solution(mesh):
    node, space = mesh.devices.shape
    cores = 2
    fine = Mesh(mesh.devices.reshape(node, space // (4 * cores), 4, cores), ("node",) + SPACE)
    placed = (P("node", SPACE, None), P(SPACE, None))
    return jax.shard_map(
        per_device, mesh=fine, in_specs=placed, out_specs=P("node", SPACE), check_vma=False
    )
```
